256 devices in a mesh: dp: 8 (over y, x_hi), expert: 8 (over z), tensor: 4 (over x_lo, core).
Axes of the slice: x: 4 (x_hi: 2, x_lo: 2; x = x_hi * 2 + x_lo), y: 4, z: 8, core: 2. Of those that a mesh axis runs over, the one named last changes fastest.
Arguments:
- tokens: bfloat16 [4096, 2048], P(('dp', 'expert', 'tensor')), may hold values from -6 to 6
- cotangent: bfloat16 [4096, 2048], P(('dp', 'expert', 'tensor')), may hold values from -3 to 3
- routes: int32 [4096, 2], P(('dp', 'expert', 'tensor')), may hold values from 0 to 7, all different within a row; in each aligned block of 16 rows (0 to 15, 16 to 31, ...) at most 5 rows name the same one
- weight_codes: int32 [4096, 2], P(('dp', 'expert', 'tensor')), may hold values from 16 to 256
- dense_gate: bfloat16 [2048, 8192], P('expert', ('dp', 'tensor')), may hold values from -0.125 to 0.125
- dense_up: bfloat16 [2048, 8192], P('expert', ('dp', 'tensor')), may hold values from -0.125 to 0.125
- dense_down_t: bfloat16 [2048, 8192], P('expert', ('dp', 'tensor')), may hold values from -0.0625 to 0.0625
Outputs:
- mixed: bfloat16 [4096, 2048], P(('dp', 'expert', 'tensor'))
- input_grad: bfloat16 [4096, 2048], P(('dp', 'expert', 'tensor'))
- grad_gate: bfloat16 [8, 2048, 8192], P('expert', None, ('dp', 'tensor'))
- grad_up: bfloat16 [8, 2048, 8192], P('expert', None, ('dp', 'tensor'))
- grad_down_t: bfloat16 [8, 2048, 8192], P('expert', None, ('dp', 'tensor'))
The draws below stay inside these ranges and needn't reach their ends.
Inputs may be any that keep to these rules, and one draw needn't show every extreme that they name: `routes`: each row names two different experts; the rows of one device name each expert at most 5 times.
All inputs are finite; a program needn't handle non-finite values.
Results may differ from the reference program's by a relative error of at most 0.02.
Values may be sent and summed in bfloat16 or wider, within the bound.
No kernel may reach another device: no remote copies, remote signals or barrier semaphores. Data moves between devices by JAX's collectives and lax.ppermute only.
A program may use at most 128 MiB of HBM per device.

```python
import math
import jax
import jax.numpy as jnp
import numpy as np
from jax import lax

D = 2048
FF = 8192
TOK_DEV = 16
EXPERTS = 8
TOKENS = 4096
CAP = 5
SLOTS = 1280
N_DP = 8
N_TENSOR = 4


def set_ends(drawn, stream_key, smallest, largest):
    longest = drawn.shape.index(max(drawn.shape))
    spots = []
    for shift in (0, 1):
        where = [jax.random.randint(jax.random.fold_in(stream_key, axis), (), 0, length) for axis, length in enumerate(drawn.shape)]
        where[longest] = (where[longest] + shift) % drawn.shape[longest]
        spots.append(tuple(where))
    return drawn.at[spots[0]].set(smallest).at[spots[1]].set(largest)


def level_of(key, shape, shards, smallest, top_value):
    gain, own = 1.0, jax.random.fold_in(key, 6)
    for position, blocks in shards:
        draws = jnp.exp(jax.random.uniform(jax.random.fold_in(own, position), (blocks,), jnp.float32, smallest / len(shards), top_value / len(shards)))
        gain = gain * jnp.repeat(draws, shape[position] // blocks).reshape([-1 if axis == position else 1 for axis in range(len(shape))])
    return gain


def assign_block(key, own, number, rows, count, top, most, slope):
    ranking = jax.random.permutation(key, count)
    crowded, ordinary = shares(count, rows * top, most, slope, True), shares(count, rows * top, most, slope, False)
    places = jnp.arange(count)

    def named(sizes, turn):
        used = int((sizes > 0).sum())
        fixed = max(1, used // 4)
        shifted = fixed + (places - fixed + turn * (used - fixed)) % max(1, count - fixed)
        return jnp.zeros((count,), jnp.int32).at[ranking[jnp.where(places < fixed, places, shifted)]].set(jnp.asarray(sizes, jnp.int32))

    sizes = jnp.where(number % 4 == 0, named(crowded, number // 4), named(ordinary, number - number // 4 - 1))
    mixed = jax.random.permutation(jax.random.fold_in(own, 3), count)
    source_of, sink = mixed[0:count // 2 * 2:2], mixed[1:count // 2 * 2:2]
    slack = jnp.minimum(sizes[source_of] - 1, most - sizes[sink]) // 2
    slack = jnp.where((source_of == ranking[0]) | (sink == ranking[0]) | (sizes[sink] == 0), 0, jnp.maximum(slack, 0))
    shifted = jax.random.randint(jax.random.fold_in(own, 4), (count // 2,), 0, 1 << 20) % (slack + 1)
    sizes = sizes.at[source_of].add(-shifted).at[sink].add(shifted)
    labels = jnp.searchsorted(jnp.cumsum(sizes), jnp.arange(rows * top), side="right").astype(jnp.int32)
    table = labels.reshape(top, rows).T
    table = table[jax.random.permutation(jax.random.fold_in(own, 1), rows)]
    turn = jax.random.randint(jax.random.fold_in(own, 2), (rows, 1), 0, top)
    return jnp.take_along_axis(table, (jnp.arange(top)[None, :] + turn) % top, axis=1)


def shares(count, total, bound, slope, full):
    weights = [(1 << 20) // math.isqrt(rank ** slope) + 1 for rank in range(1, count + 1)]
    largest = bound if full else min(bound, max(-(-total // count), total * weights[0] // sum(weights)))
    least = 1 if total - largest >= count - 1 else 0
    given, rest = [largest] + [least] * (count - 1), total - largest - least * (count - 1)
    while rest > 0:
        free = [i for i in range(1, count) if given[i] < largest] or [i for i in range(1, count) if given[i] < bound]
        pool, remaining = sum([weights[i] for i in free]), rest
        for i in free:
            extra = min(bound - given[i], max(1, remaining * weights[i] // pool), rest)
            given[i] = given[i] + extra
            rest = rest - extra
    return np.array(given)


def normal_values(own_key, dims, deviation, limit, pieces=(), kind=jnp.bfloat16):
    drawn = jax.random.normal(own_key, dims, jnp.float32) * deviation
    if len(pieces) > 0:
        drawn = level_of(own_key, dims, pieces, -0.22, 0.18) * drawn
    return jnp.clip(drawn, min=-limit, max=limit).astype(kind)


def setup_inputs(seed: int = 0) -> dict:
    key_of = jax.random.split(jax.random.key(seed), 8)
    tokens = normal_values(key_of[0], (TOKENS, D), 1.0, 6.0, ((0, 256),))
    cotangent = normal_values(key_of[1], (TOKENS, D), 0.5, 3.0, ((0, 256),))
    routes_keys = jax.random.split(jax.random.fold_in(key_of[2], 1), TOKENS // TOK_DEV)
    routes_turns = jax.random.permutation(jax.random.fold_in(key_of[2], 3), TOKENS // TOK_DEV)
    routes = jax.vmap(lambda own, number: assign_block(jax.random.fold_in(key_of[2], 2), own, number, TOK_DEV, EXPERTS, 2, CAP, 2))(routes_keys, routes_turns).reshape((TOKENS, 2))
    weight_codes = set_ends(jax.random.randint(key_of[3], (TOKENS, 2), 16, 257), jax.random.fold_in(key_of[3], 1), 16, 256).astype(jnp.int32)
    dense_gate = normal_values(key_of[4], (D, FF), D ** -0.5, 0.125, ((0, 8), (1, 32)))
    dense_up = normal_values(key_of[5], (D, FF), D ** -0.5, 0.125, ((0, 8), (1, 32)))
    dense_down_t = normal_values(key_of[6], (D, FF), FF ** -0.5, 0.0625, ((0, 8), (1, 32)))
    return dict(tokens=tokens, cotangent=cotangent, routes=routes, weight_codes=weight_codes, dense_gate=dense_gate, dense_up=dense_up, dense_down_t=dense_down_t)


def silu_parts(gate_pre):
    sigmoid_val = jax.nn.sigmoid(gate_pre)
    return gate_pre * sigmoid_val, sigmoid_val * (1.0 + gate_pre * (1.0 - sigmoid_val))


def contract_rows(left_side, right_side):
    return lax.dot_general(left_side, right_side, (((0,), (0,)), ((), ())), preferred_element_type=jnp.float32)


def contract_cols(left_side, right_side):
    return lax.dot_general(left_side, right_side, (((1,), (1,)), ((), ())), preferred_element_type=jnp.float32)


def block_sum(left_parts, right_parts):
    hid_width = FF // (N_DP * N_TENSOR)

    def add_block(block_index, running):
        col_start = (block_index * hid_width).astype(jnp.int32)
        block_term = jnp.zeros((TOKENS, D), jnp.float32)
        for left_side, right_side in zip(left_parts, right_parts):
            block_term = block_term + contract_cols(
                lax.dynamic_slice_in_dim(left_side, col_start, hid_width, 1),
                lax.dynamic_slice_in_dim(right_side, col_start, hid_width, 1))
        rounded = lax.optimization_barrier(block_term.astype(jnp.bfloat16))
        return running + rounded.astype(jnp.float32)

    total_sum = lax.fori_loop(jnp.int32(0), jnp.int32(N_DP * N_TENSOR), add_block, jnp.zeros((TOKENS, D), jnp.float32))
    return total_sum.astype(jnp.bfloat16)


def reference(tokens, cotangent, routes, weight_codes, dense_gate, dense_up, dense_down_t):
    code_scale = weight_codes.astype(jnp.float32) / 256.0
    gate_pre = jnp.dot(tokens, dense_gate, preferred_element_type=jnp.float32)
    up_pre = jnp.dot(tokens, dense_up, preferred_element_type=jnp.float32)
    activation, act_slope = silu_parts(gate_pre)
    hidden = (activation * up_pre).astype(jnp.bfloat16)
    expert_out = block_sum((hidden,), (dense_down_t,)).astype(jnp.float32)
    mixed = (code_scale[:, 0:1] * expert_out + code_scale[:, 1:2] * expert_out).astype(jnp.bfloat16)
    scaled_list = []
    gate_list = []
    up_list = []
    input_sum = jnp.zeros((TOKENS, D), jnp.float32)
    for which in range(2):
        scaled = (code_scale[:, which:which + 1] * cotangent.astype(jnp.float32)).astype(jnp.bfloat16)
        hidden_grad = jnp.dot(scaled, dense_down_t, preferred_element_type=jnp.float32)
        gate_grad = (hidden_grad * up_pre * act_slope).astype(jnp.bfloat16)
        up_grad = (hidden_grad * activation).astype(jnp.bfloat16)
        input_sum = input_sum + block_sum((gate_grad, up_grad), (dense_gate, dense_up)).astype(jnp.float32)
        scaled_list.append(scaled)
        gate_list.append(gate_grad)
        up_list.append(up_grad)
    input_grad = input_sum.astype(jnp.bfloat16)
    flat_route = routes.reshape(-1)
    flat_tokens = jnp.repeat(tokens, 2, axis=0)
    flat_hidden = jnp.repeat(hidden, 2, axis=0)
    flat_scaled = jnp.stack(scaled_list, axis=1).reshape(2 * TOKENS, D)
    flat_gate = jnp.stack(gate_list, axis=1).reshape(2 * TOKENS, FF)
    flat_up = jnp.stack(up_list, axis=1).reshape(2 * TOKENS, FF)

    def one_expert(expert_id):
        chosen = flat_route == expert_id
        picked = jnp.nonzero(chosen, size=SLOTS, fill_value=0)[0]
        valid = (jnp.arange(SLOTS) < jnp.sum(chosen.astype(jnp.int32))).astype(jnp.bfloat16)[:, None]
        rows_x = flat_tokens[picked] * valid
        rows_scaled = flat_scaled[picked] * valid
        return (contract_rows(rows_x, flat_gate[picked]).astype(jnp.bfloat16),
                contract_rows(rows_x, flat_up[picked]).astype(jnp.bfloat16),
                contract_rows(rows_scaled, flat_hidden[picked]).astype(jnp.bfloat16))

    grad_gate, grad_up, grad_down_t = lax.map(one_expert, jnp.arange(EXPERTS, dtype=jnp.int32))
    return (mixed, input_grad, grad_gate, grad_up, grad_down_t)
```

```python
import jax
import jax.numpy as jnp
from jax import lax
from jax.sharding import PartitionSpec as P

GROUP = ("dp", "tensor")


def silu_parts(gate_pre):
    sigmoid_val = jax.nn.sigmoid(gate_pre)
    return (gate_pre * sigmoid_val, sigmoid_val * (1.0 + gate_pre * (1.0 - sigmoid_val)))


def contract_rows(left_side, right_side):
    return lax.dot_general(
        left_side, right_side, (((0,), (0,)), ((), ())), preferred_element_type=jnp.float32
    )


def contract_cols(left_side, right_side):
    return lax.dot_general(
        left_side, right_side, (((1,), (1,)), ((), ())), preferred_element_type=jnp.float32
    )


def forward_parts(rows_x, gate_cols, up_cols):
    gate_pre = jnp.dot(rows_x, gate_cols, preferred_element_type=jnp.float32)
    up_pre = jnp.dot(rows_x, up_cols, preferred_element_type=jnp.float32)
    activation, act_slope = silu_parts(gate_pre)
    hidden = (activation * up_pre).astype(jnp.bfloat16)
    return up_pre, activation, act_slope, hidden


def grad_parts(scaled, down_cols, up_pre, activation, act_slope):
    hidden_grad = jnp.dot(scaled, down_cols, preferred_element_type=jnp.float32)
    gate_grad = (hidden_grad * up_pre * act_slope).astype(jnp.bfloat16)
    up_grad = (hidden_grad * activation).astype(jnp.bfloat16)
    return gate_grad, up_grad


def shards(tokens, cotangent, routes, weight_codes, dense_gate, dense_up, dense_down_t):
    experts = lax.axis_size("expert")
    count_tok, model_width = tokens.shape
    hid = dense_gate.shape[1]
    capacity = 5 * count_tok // (2 * experts)
    slots_here = experts * capacity

    stacked = jnp.concatenate([dense_gate, dense_up, dense_down_t], axis=1)
    full_cols = lax.all_gather(stacked, "expert", axis=0, tiled=True)
    gate_cols = full_cols[:, :hid]
    up_cols = full_cols[:, hid : 2 * hid]
    down_cols = full_cols[:, 2 * hid :]
    gate_up_cols = full_cols[:, : 2 * hid]

    code_cols = jnp.zeros((count_tok, 128), jnp.bfloat16)
    code_cols = code_cols.at[:, 0:2].set(weight_codes.astype(jnp.bfloat16))
    home = jnp.concatenate([tokens, cotangent, code_cols], axis=1)
    plane = lax.all_gather(home, GROUP, axis=0, tiled=True)
    plane_x = plane[:, :model_width]
    plane_dy = plane[:, model_width : 2 * model_width].astype(jnp.float32)
    plane_scale = plane[:, 2 * model_width : 2 * model_width + 2].astype(jnp.float32) / 256.0

    up_pre, activation, act_slope, hidden = forward_parts(plane_x, gate_cols, up_cols)
    out_term = contract_cols(hidden, down_cols).astype(jnp.bfloat16)
    grad_term = jnp.zeros(out_term.shape, jnp.float32)
    for which in range(2):
        scaled = (plane_scale[:, which : which + 1] * plane_dy).astype(jnp.bfloat16)
        gate_grad, up_grad = grad_parts(scaled, down_cols, up_pre, activation, act_slope)
        grad_term = grad_term + contract_cols(
            jnp.concatenate([gate_grad, up_grad], axis=1), gate_up_cols
        )
    terms = jnp.concatenate([out_term, grad_term.astype(jnp.bfloat16)], axis=1)
    summed = lax.psum_scatter(terms, GROUP, scatter_dimension=0, tiled=True)
    expert_out = summed[:, :model_width].astype(jnp.float32)
    code_scale = weight_codes.astype(jnp.float32) / 256.0
    mixed = (code_scale[:, 0:1] * expert_out + code_scale[:, 1:2] * expert_out).astype(
        jnp.bfloat16
    )
    input_grad = summed[:, model_width:]

    flat_route = routes.reshape(-1)
    flat_scale = weight_codes.reshape(-1).astype(jnp.float32) / 256.0
    onehot = (flat_route[:, None] == jnp.arange(experts, dtype=jnp.int32)[None, :]).astype(
        jnp.int32
    )
    earlier = jnp.cumsum(onehot, axis=0) - onehot
    slot_of = flat_route * capacity + jnp.sum(earlier * onehot, axis=1)
    placed = (slot_of[None, :] == jnp.arange(slots_here, dtype=jnp.int32)[:, None]).astype(
        jnp.bfloat16
    )
    flat_x = jnp.repeat(tokens, 2, axis=0)
    flat_scaled = (flat_scale[:, None] * jnp.repeat(cotangent, 2, axis=0).astype(jnp.float32)).astype(
        jnp.bfloat16
    )
    send_x = jnp.dot(placed, flat_x, preferred_element_type=jnp.float32).astype(jnp.bfloat16)
    send_s = jnp.dot(placed, flat_scaled, preferred_element_type=jnp.float32).astype(jnp.bfloat16)
    send = jnp.stack(
        [send_x.reshape(experts, capacity, model_width), send_s.reshape(experts, capacity, model_width)],
        axis=1,
    )
    got = lax.all_to_all(send, "expert", split_axis=0, concat_axis=0, tiled=True)
    got = jnp.transpose(got, (1, 0, 2, 3))
    rows = lax.all_gather(got, GROUP, axis=1, tiled=True)
    rows_x = rows[0].reshape(-1, model_width)
    rows_s = rows[1].reshape(-1, model_width)
    r_up, r_act, r_slope, r_hidden = forward_parts(rows_x, gate_cols, up_cols)
    r_gate, r_upg = grad_parts(rows_s, down_cols, r_up, r_act, r_slope)
    grad_gate = contract_rows(rows_x, r_gate).astype(jnp.bfloat16)[None]
    grad_up = contract_rows(rows_x, r_upg).astype(jnp.bfloat16)[None]
    grad_down_t = contract_rows(rows_s, r_hidden).astype(jnp.bfloat16)[None]
    return (mixed, input_grad, grad_gate, grad_up, grad_down_t)


def solution(mesh):
    rows = P(("dp", "expert", "tensor"), None)
    weights = P("expert", ("dp", "tensor"))
    grads = P("expert", None, ("dp", "tensor"))
    return jax.shard_map(
        shards,
        mesh=mesh,
        in_specs=(rows, rows, rows, rows, weights, weights, weights),
        out_specs=(rows, rows, grads, grads, grads),
        check_vma=False,
    )
```

```python
import jax
import jax.numpy as jnp
from jax import lax
from jax.sharding import PartitionSpec as P

GROUP = ("dp", "tensor")


def silu_parts(gate_pre):
    sigmoid_val = jax.nn.sigmoid(gate_pre)
    return (gate_pre * sigmoid_val, sigmoid_val * (1.0 + gate_pre * (1.0 - sigmoid_val)))


def contract_rows(left_side, right_side):
    return lax.dot_general(
        left_side, right_side, (((0,), (0,)), ((), ())), preferred_element_type=jnp.float32
    )


def contract_cols(left_side, right_side):
    return lax.dot_general(
        left_side, right_side, (((1,), (1,)), ((), ())), preferred_element_type=jnp.float32
    )


def forward_parts(rows_x, gate_cols, up_cols):
    gate_pre = jnp.dot(rows_x, gate_cols, preferred_element_type=jnp.float32)
    up_pre = jnp.dot(rows_x, up_cols, preferred_element_type=jnp.float32)
    activation, act_slope = silu_parts(gate_pre)
    hidden = (activation * up_pre).astype(jnp.bfloat16)
    return up_pre, activation, act_slope, hidden


def grad_parts(scaled, down_cols, up_pre, activation, act_slope):
    hidden_grad = jnp.dot(scaled, down_cols, preferred_element_type=jnp.float32)
    gate_grad = (hidden_grad * up_pre * act_slope).astype(jnp.bfloat16)
    up_grad = (hidden_grad * activation).astype(jnp.bfloat16)
    return gate_grad, up_grad


def shards(tokens, cotangent, routes, weight_codes, dense_gate, dense_up, dense_down_t):
    experts = lax.axis_size("expert")
    count_tok, model_width = tokens.shape
    hid = dense_gate.shape[1]
    capacity = 5 * count_tok // (2 * experts)
    slots_here = experts * capacity

    stacked = jnp.concatenate([dense_gate, dense_up, dense_down_t], axis=1)
    full_cols = lax.all_gather(stacked, "expert", axis=0, tiled=True)
    gate_cols = full_cols[:, :hid]
    up_cols = full_cols[:, hid : 2 * hid]
    down_cols = full_cols[:, 2 * hid :]
    gate_up_cols = full_cols[:, : 2 * hid]

    code_cols = jnp.zeros((count_tok, 128), jnp.bfloat16)
    code_cols = code_cols.at[:, 0:2].set(weight_codes.astype(jnp.bfloat16))
    home = jnp.concatenate([tokens, cotangent, code_cols], axis=1)
    plane = lax.all_gather(home, GROUP, axis=0, tiled=True)
    plane_x = plane[:, :model_width]
    plane_dy = plane[:, model_width : 2 * model_width].astype(jnp.float32)
    plane_scale = plane[:, 2 * model_width : 2 * model_width + 2].astype(jnp.float32) / 256.0

    up_pre, activation, act_slope, hidden = forward_parts(plane_x, gate_cols, up_cols)
    out_term = contract_cols(hidden, down_cols).astype(jnp.bfloat16)
    grad_term = jnp.zeros(out_term.shape, jnp.float32)
    for which in range(2):
        scaled = (plane_scale[:, which : which + 1] * plane_dy).astype(jnp.bfloat16)
        gate_grad, up_grad = grad_parts(scaled, down_cols, up_pre, activation, act_slope)
        grad_term = grad_term + contract_cols(
            jnp.concatenate([gate_grad, up_grad], axis=1), gate_up_cols
        )
    terms = jnp.concatenate([out_term, grad_term.astype(jnp.bfloat16)], axis=1)

    flat_route = routes.reshape(-1)
    flat_scale = weight_codes.reshape(-1).astype(jnp.float32) / 256.0
    onehot = (flat_route[:, None] == jnp.arange(experts, dtype=jnp.int32)[None, :]).astype(
        jnp.int32
    )
    earlier = jnp.cumsum(onehot, axis=0) - onehot
    slot_of = flat_route * capacity + jnp.sum(earlier * onehot, axis=1)
    placed = (slot_of[None, :] == jnp.arange(slots_here, dtype=jnp.int32)[:, None]).astype(
        jnp.bfloat16
    )
    flat_x = jnp.repeat(tokens, 2, axis=0)
    flat_scaled = (flat_scale[:, None] * jnp.repeat(cotangent, 2, axis=0).astype(jnp.float32)).astype(
        jnp.bfloat16
    )
    send_x = jnp.dot(placed, flat_x, preferred_element_type=jnp.float32).astype(jnp.bfloat16)
    send_s = jnp.dot(placed, flat_scaled, preferred_element_type=jnp.float32).astype(jnp.bfloat16)
    send = jnp.concatenate([send_x, send_s], axis=1)
    got = lax.all_to_all(send, "expert", split_axis=0, concat_axis=0, tiled=True)
    rows = lax.all_gather(got, GROUP, axis=0, tiled=True)
    terms, rows = lax.optimization_barrier((terms, rows))
    summed = lax.psum_scatter(terms, GROUP, scatter_dimension=0, tiled=True)
    expert_out = summed[:, :model_width].astype(jnp.float32)
    code_scale = weight_codes.astype(jnp.float32) / 256.0
    mixed = (code_scale[:, 0:1] * expert_out + code_scale[:, 1:2] * expert_out).astype(
        jnp.bfloat16
    )
    input_grad = summed[:, model_width:]
    rows_x = rows[:, :model_width]
    rows_s = rows[:, model_width:]
    r_up, r_act, r_slope, r_hidden = forward_parts(rows_x, gate_cols, up_cols)
    r_gate, r_upg = grad_parts(rows_s, down_cols, r_up, r_act, r_slope)
    grad_gate = contract_rows(rows_x, r_gate).astype(jnp.bfloat16)[None]
    grad_up = contract_rows(rows_x, r_upg).astype(jnp.bfloat16)[None]
    grad_down_t = contract_rows(rows_s, r_hidden).astype(jnp.bfloat16)[None]
    return (mixed, input_grad, grad_gate, grad_up, grad_down_t)


def solution(mesh):
    rows = P(("dp", "expert", "tensor"), None)
    weights = P("expert", ("dp", "tensor"))
    grads = P("expert", None, ("dp", "tensor"))
    return jax.shard_map(
        shards,
        mesh=mesh,
        in_specs=(rows, rows, rows, rows, weights, weights, weights),
        out_specs=(rows, rows, grads, grads, grads),
        check_vma=False,
    )
```

```python
import jax
import jax.numpy as jnp
from jax import lax
from jax.sharding import PartitionSpec as P

GROUP = ("dp", "tensor")


def silu_parts(gate_pre):
    sigmoid_val = jax.nn.sigmoid(gate_pre)
    return (gate_pre * sigmoid_val, sigmoid_val * (1.0 + gate_pre * (1.0 - sigmoid_val)))


def contract_rows(left_side, right_side):
    return lax.dot_general(
        left_side, right_side, (((0,), (0,)), ((), ())), preferred_element_type=jnp.float32
    )


def contract_cols(left_side, right_side):
    return lax.dot_general(
        left_side, right_side, (((1,), (1,)), ((), ())), preferred_element_type=jnp.float32
    )


def forward_parts(rows_x, gate_cols, up_cols):
    gate_pre = jnp.dot(rows_x, gate_cols, preferred_element_type=jnp.float32)
    up_pre = jnp.dot(rows_x, up_cols, preferred_element_type=jnp.float32)
    activation, act_slope = silu_parts(gate_pre)
    hidden = (activation * up_pre).astype(jnp.bfloat16)
    return up_pre, activation, act_slope, hidden


def grad_parts(scaled, down_cols, up_pre, activation, act_slope):
    hidden_grad = jnp.dot(scaled, down_cols, preferred_element_type=jnp.float32)
    gate_grad = (hidden_grad * up_pre * act_slope).astype(jnp.bfloat16)
    up_grad = (hidden_grad * activation).astype(jnp.bfloat16)
    return gate_grad, up_grad


def shards(tokens, cotangent, routes, weight_codes, dense_gate, dense_up, dense_down_t):
    experts = lax.axis_size("expert")
    count_tok, model_width = tokens.shape
    hid = dense_gate.shape[1]
    capacity = 5 * count_tok // (2 * experts)
    slots_here = experts * capacity

    stacked = jnp.concatenate([dense_gate, dense_up, dense_down_t], axis=1)
    full_cols = lax.all_gather(stacked, "expert", axis=0, tiled=True)
    gate_cols = full_cols[:, :hid]
    up_cols = full_cols[:, hid : 2 * hid]
    down_cols = full_cols[:, 2 * hid :]
    gate_up_cols = full_cols[:, : 2 * hid]

    flat_route = routes.reshape(-1)
    flat_scale = weight_codes.reshape(-1).astype(jnp.float32) / 256.0
    onehot = (flat_route[:, None] == jnp.arange(experts, dtype=jnp.int32)[None, :]).astype(
        jnp.int32
    )
    earlier = jnp.cumsum(onehot, axis=0) - onehot
    slot_of = flat_route * capacity + jnp.sum(earlier * onehot, axis=1)
    placed = (slot_of[None, :] == jnp.arange(slots_here, dtype=jnp.int32)[:, None]).astype(
        jnp.bfloat16
    )
    flat_x = jnp.repeat(tokens, 2, axis=0)
    flat_scaled = (flat_scale[:, None] * jnp.repeat(cotangent, 2, axis=0).astype(jnp.float32)).astype(
        jnp.bfloat16
    )
    send_x = jnp.dot(placed, flat_x, preferred_element_type=jnp.float32).astype(jnp.bfloat16)
    send_s = jnp.dot(placed, flat_scaled, preferred_element_type=jnp.float32).astype(jnp.bfloat16)
    send = jnp.concatenate([send_x, send_s], axis=1)
    got = lax.all_to_all(send, "expert", split_axis=0, concat_axis=0, tiled=True)

    code_rows = jnp.zeros((8, 2 * model_width), jnp.bfloat16)
    code_rows = code_rows.at[0, : 2 * count_tok].set(weight_codes.reshape(-1).astype(jnp.bfloat16))
    parcel = jnp.concatenate(
        [got, jnp.concatenate([tokens, cotangent], axis=1), code_rows], axis=0
    )
    per_dev = parcel.shape[0]
    full_cols, parcel = lax.optimization_barrier((full_cols, parcel))
    gate_cols = full_cols[:, :hid]
    up_cols = full_cols[:, hid : 2 * hid]
    down_cols = full_cols[:, 2 * hid :]
    gate_up_cols = full_cols[:, : 2 * hid]
    gathered = lax.all_gather(parcel, ("tensor", "dp"), axis=0, tiled=True)
    gathered = gathered.reshape(-1, per_dev, 2 * model_width)
    rows = gathered[:, :slots_here].reshape(-1, 2 * model_width)
    plane = gathered[:, slots_here : slots_here + count_tok].reshape(-1, 2 * model_width)
    plane_codes = gathered[:, slots_here + count_tok, : 2 * count_tok].reshape(-1, 2)
    plane_x = plane[:, :model_width]
    plane_dy = plane[:, model_width:].astype(jnp.float32)
    plane_scale = plane_codes.astype(jnp.float32) / 256.0

    up_pre, activation, act_slope, hidden = forward_parts(plane_x, gate_cols, up_cols)
    out_term = contract_cols(hidden, down_cols).astype(jnp.bfloat16)
    grad_term = jnp.zeros(out_term.shape, jnp.float32)
    for which in range(2):
        scaled = (plane_scale[:, which : which + 1] * plane_dy).astype(jnp.bfloat16)
        gate_grad, up_grad = grad_parts(scaled, down_cols, up_pre, activation, act_slope)
        grad_term = grad_term + contract_cols(
            jnp.concatenate([gate_grad, up_grad], axis=1), gate_up_cols
        )
    terms = jnp.concatenate([out_term, grad_term.astype(jnp.bfloat16)], axis=1)
    part = lax.psum_scatter(terms, "tensor", scatter_dimension=0, tiled=True)
    summed = lax.psum_scatter(part, "dp", scatter_dimension=0, tiled=True)
    expert_out = summed[:, :model_width].astype(jnp.float32)
    code_scale = weight_codes.astype(jnp.float32) / 256.0
    mixed = (code_scale[:, 0:1] * expert_out + code_scale[:, 1:2] * expert_out).astype(
        jnp.bfloat16
    )
    input_grad = summed[:, model_width:]
    rows_x = rows[:, :model_width]
    rows_s = rows[:, model_width:]
    r_up, r_act, r_slope, r_hidden = forward_parts(rows_x, gate_cols, up_cols)
    r_gate, r_upg = grad_parts(rows_s, down_cols, r_up, r_act, r_slope)
    grad_gate = contract_rows(rows_x, r_gate).astype(jnp.bfloat16)[None]
    grad_up = contract_rows(rows_x, r_upg).astype(jnp.bfloat16)[None]
    grad_down_t = contract_rows(rows_s, r_hidden).astype(jnp.bfloat16)[None]
    return (mixed, input_grad, grad_gate, grad_up, grad_down_t)


def solution(mesh):
    rows = P(("dp", "expert", "tensor"), None)
    weights = P("expert", ("dp", "tensor"))
    grads = P("expert", None, ("dp", "tensor"))
    return jax.shard_map(
        shards,
        mesh=mesh,
        in_specs=(rows, rows, rows, rows, weights, weights, weights),
        out_specs=(rows, rows, grads, grads, grads),
        check_vma=False,
    )
```

```python
import jax
import jax.numpy as jnp
from jax import lax
from jax.sharding import PartitionSpec as P

GROUP = ("dp", "tensor")


def silu_parts(gate_pre):
    sigmoid_val = jax.nn.sigmoid(gate_pre)
    return (gate_pre * sigmoid_val, sigmoid_val * (1.0 + gate_pre * (1.0 - sigmoid_val)))


def contract_rows(left_side, right_side):
    return lax.dot_general(
        left_side, right_side, (((0,), (0,)), ((), ())), preferred_element_type=jnp.float32
    )


def contract_cols(left_side, right_side):
    return lax.dot_general(
        left_side, right_side, (((1,), (1,)), ((), ())), preferred_element_type=jnp.float32
    )


def forward_parts(rows_x, gate_cols, up_cols):
    gate_pre = jnp.dot(rows_x, gate_cols, preferred_element_type=jnp.float32)
    up_pre = jnp.dot(rows_x, up_cols, preferred_element_type=jnp.float32)
    activation, act_slope = silu_parts(gate_pre)
    hidden = (activation * up_pre).astype(jnp.bfloat16)
    return up_pre, activation, act_slope, hidden


def grad_parts(scaled, down_cols, up_pre, activation, act_slope):
    hidden_grad = jnp.dot(scaled, down_cols, preferred_element_type=jnp.float32)
    gate_grad = (hidden_grad * up_pre * act_slope).astype(jnp.bfloat16)
    up_grad = (hidden_grad * activation).astype(jnp.bfloat16)
    return gate_grad, up_grad


def shards(tokens, cotangent, routes, weight_codes, dense_gate, dense_up, dense_down_t):
    experts = lax.axis_size("expert")
    count_tok, model_width = tokens.shape
    hid = dense_gate.shape[1]
    capacity = 5 * count_tok // (2 * experts)
    slots_here = experts * capacity

    stacked = jnp.concatenate([dense_gate, dense_up, dense_down_t], axis=1)
    copies = jnp.broadcast_to(stacked[None], (experts,) + stacked.shape)
    full_cols = lax.all_to_all(copies, "expert", split_axis=0, concat_axis=0, tiled=True)
    full_cols = full_cols.reshape(-1, stacked.shape[1])
    gate_cols = full_cols[:, :hid]
    up_cols = full_cols[:, hid : 2 * hid]
    down_cols = full_cols[:, 2 * hid :]
    gate_up_cols = full_cols[:, : 2 * hid]

    code_cols = jnp.zeros((count_tok, 128), jnp.bfloat16)
    code_cols = code_cols.at[:, 0:2].set(weight_codes.astype(jnp.bfloat16))
    home = jnp.concatenate([tokens, cotangent, code_cols], axis=1)
    plane = lax.all_gather(home, GROUP, axis=0, tiled=True)
    plane_x = plane[:, :model_width]
    plane_dy = plane[:, model_width : 2 * model_width].astype(jnp.float32)
    plane_scale = plane[:, 2 * model_width : 2 * model_width + 2].astype(jnp.float32) / 256.0

    up_pre, activation, act_slope, hidden = forward_parts(plane_x, gate_cols, up_cols)
    out_term = contract_cols(hidden, down_cols).astype(jnp.bfloat16)
    grad_term = jnp.zeros(out_term.shape, jnp.float32)
    for which in range(2):
        scaled = (plane_scale[:, which : which + 1] * plane_dy).astype(jnp.bfloat16)
        gate_grad, up_grad = grad_parts(scaled, down_cols, up_pre, activation, act_slope)
        grad_term = grad_term + contract_cols(
            jnp.concatenate([gate_grad, up_grad], axis=1), gate_up_cols
        )
    terms = jnp.concatenate([out_term, grad_term.astype(jnp.bfloat16)], axis=1)

    flat_route = routes.reshape(-1)
    flat_scale = weight_codes.reshape(-1).astype(jnp.float32) / 256.0
    onehot = (flat_route[:, None] == jnp.arange(experts, dtype=jnp.int32)[None, :]).astype(
        jnp.int32
    )
    earlier = jnp.cumsum(onehot, axis=0) - onehot
    slot_of = flat_route * capacity + jnp.sum(earlier * onehot, axis=1)
    placed = (slot_of[None, :] == jnp.arange(slots_here, dtype=jnp.int32)[:, None]).astype(
        jnp.bfloat16
    )
    flat_x = jnp.repeat(tokens, 2, axis=0)
    flat_scaled = (flat_scale[:, None] * jnp.repeat(cotangent, 2, axis=0).astype(jnp.float32)).astype(
        jnp.bfloat16
    )
    send_x = jnp.dot(placed, flat_x, preferred_element_type=jnp.float32).astype(jnp.bfloat16)
    send_s = jnp.dot(placed, flat_scaled, preferred_element_type=jnp.float32).astype(jnp.bfloat16)
    send = jnp.concatenate([send_x, send_s], axis=1)
    got = lax.all_to_all(send, "expert", split_axis=0, concat_axis=0, tiled=True)
    rows = lax.all_gather(got, GROUP, axis=0, tiled=True)
    terms, rows = lax.optimization_barrier((terms, rows))
    summed = lax.psum_scatter(terms, GROUP, scatter_dimension=0, tiled=True)
    expert_out = summed[:, :model_width].astype(jnp.float32)
    code_scale = weight_codes.astype(jnp.float32) / 256.0
    mixed = (code_scale[:, 0:1] * expert_out + code_scale[:, 1:2] * expert_out).astype(
        jnp.bfloat16
    )
    input_grad = summed[:, model_width:]
    rows_x = rows[:, :model_width]
    rows_s = rows[:, model_width:]
    r_up, r_act, r_slope, r_hidden = forward_parts(rows_x, gate_cols, up_cols)
    r_gate, r_upg = grad_parts(rows_s, down_cols, r_up, r_act, r_slope)
    grad_gate = contract_rows(rows_x, r_gate).astype(jnp.bfloat16)[None]
    grad_up = contract_rows(rows_x, r_upg).astype(jnp.bfloat16)[None]
    grad_down_t = contract_rows(rows_s, r_hidden).astype(jnp.bfloat16)[None]
    return (mixed, input_grad, grad_gate, grad_up, grad_down_t)


def solution(mesh):
    rows = P(("dp", "expert", "tensor"), None)
    weights = P("expert", ("dp", "tensor"))
    grads = P("expert", None, ("dp", "tensor"))
    return jax.shard_map(
        shards,
        mesh=mesh,
        in_specs=(rows, rows, rows, rows, weights, weights, weights),
        out_specs=(rows, rows, grads, grads, grads),
        check_vma=False,
    )
```

```python
import jax
import jax.numpy as jnp
from jax import lax
from jax.sharding import PartitionSpec as P

GROUP = ("dp", "tensor")


def silu_parts(gate_pre):
    sigmoid_val = jax.nn.sigmoid(gate_pre)
    return (gate_pre * sigmoid_val, sigmoid_val * (1.0 + gate_pre * (1.0 - sigmoid_val)))


def contract_rows(left_side, right_side):
    return lax.dot_general(
        left_side, right_side, (((0,), (0,)), ((), ())), preferred_element_type=jnp.float32
    )


def contract_cols(left_side, right_side):
    return lax.dot_general(
        left_side, right_side, (((1,), (1,)), ((), ())), preferred_element_type=jnp.float32
    )


def forward_parts(rows_x, gate_cols, up_cols):
    gate_pre = jnp.dot(rows_x, gate_cols, preferred_element_type=jnp.float32)
    up_pre = jnp.dot(rows_x, up_cols, preferred_element_type=jnp.float32)
    activation, act_slope = silu_parts(gate_pre)
    hidden = (activation * up_pre).astype(jnp.bfloat16)
    return up_pre, activation, act_slope, hidden


def grad_parts(scaled, down_cols, up_pre, activation, act_slope):
    hidden_grad = jnp.dot(scaled, down_cols, preferred_element_type=jnp.float32)
    gate_grad = (hidden_grad * up_pre * act_slope).astype(jnp.bfloat16)
    up_grad = (hidden_grad * activation).astype(jnp.bfloat16)
    return gate_grad, up_grad


def shards(tokens, cotangent, routes, weight_codes, dense_gate, dense_up, dense_down_t):
    experts = lax.axis_size("expert")
    count_tok, model_width = tokens.shape
    hid = dense_gate.shape[1]
    capacity = 5 * count_tok // (2 * experts)
    slots_here = experts * capacity

    stacked = jnp.concatenate([dense_gate, dense_up, dense_down_t], axis=1)
    copies = jnp.broadcast_to(stacked[None], (experts,) + stacked.shape)
    full_cols = lax.all_to_all(copies, "expert", split_axis=0, concat_axis=0, tiled=True)
    full_cols = full_cols.reshape(-1, stacked.shape[1])
    gate_cols = full_cols[:, :hid]
    up_cols = full_cols[:, hid : 2 * hid]
    down_cols = full_cols[:, 2 * hid :]
    gate_up_cols = full_cols[:, : 2 * hid]

    code_cols = jnp.zeros((count_tok, 128), jnp.bfloat16)
    code_cols = code_cols.at[:, 0:2].set(weight_codes.astype(jnp.bfloat16))
    home = jnp.concatenate([tokens, cotangent, code_cols], axis=1)
    plane = lax.all_gather(home, GROUP, axis=0, tiled=True)
    plane_x = plane[:, :model_width]
    plane_dy = plane[:, model_width : 2 * model_width].astype(jnp.float32)
    plane_scale = plane[:, 2 * model_width : 2 * model_width + 2].astype(jnp.float32) / 256.0

    up_pre, activation, act_slope, hidden = forward_parts(plane_x, gate_cols, up_cols)
    out_term = contract_cols(hidden, down_cols).astype(jnp.bfloat16)
    grad_term = jnp.zeros(out_term.shape, jnp.float32)
    for which in range(2):
        scaled = (plane_scale[:, which : which + 1] * plane_dy).astype(jnp.bfloat16)
        gate_grad, up_grad = grad_parts(scaled, down_cols, up_pre, activation, act_slope)
        grad_term = grad_term + contract_cols(
            jnp.concatenate([gate_grad, up_grad], axis=1), gate_up_cols
        )
    terms = jnp.concatenate([out_term, grad_term.astype(jnp.bfloat16)], axis=1)

    flat_route = routes.reshape(-1)
    flat_scale = weight_codes.reshape(-1).astype(jnp.float32) / 256.0
    onehot = (flat_route[:, None] == jnp.arange(experts, dtype=jnp.int32)[None, :]).astype(
        jnp.int32
    )
    earlier = jnp.cumsum(onehot, axis=0) - onehot
    slot_of = flat_route * capacity + jnp.sum(earlier * onehot, axis=1)
    placed = (slot_of[None, :] == jnp.arange(slots_here, dtype=jnp.int32)[:, None]).astype(
        jnp.bfloat16
    )
    flat_x = jnp.repeat(tokens, 2, axis=0)
    flat_scaled = (flat_scale[:, None] * jnp.repeat(cotangent, 2, axis=0).astype(jnp.float32)).astype(
        jnp.bfloat16
    )
    send_x = jnp.dot(placed, flat_x, preferred_element_type=jnp.float32).astype(jnp.bfloat16)
    send_s = jnp.dot(placed, flat_scaled, preferred_element_type=jnp.float32).astype(jnp.bfloat16)
    send = jnp.concatenate([send_x, send_s], axis=1)
    got = lax.all_to_all(send, "expert", split_axis=0, concat_axis=0, tiled=True)
    rows = lax.all_gather(got, GROUP, axis=0, tiled=True)
    n_group = terms.shape[0] // count_tok
    pieces = terms.reshape(n_group, count_tok, 2 * model_width)
    pieces = lax.all_to_all(pieces, GROUP, split_axis=0, concat_axis=0, tiled=True)
    summed = jnp.sum(pieces.astype(jnp.float32), axis=0)
    expert_out = summed[:, :model_width].astype(jnp.bfloat16).astype(jnp.float32)
    code_scale = weight_codes.astype(jnp.float32) / 256.0
    mixed = (code_scale[:, 0:1] * expert_out + code_scale[:, 1:2] * expert_out).astype(
        jnp.bfloat16
    )
    input_grad = summed[:, model_width:].astype(jnp.bfloat16)
    rows_x = rows[:, :model_width]
    rows_s = rows[:, model_width:]
    r_up, r_act, r_slope, r_hidden = forward_parts(rows_x, gate_cols, up_cols)
    r_gate, r_upg = grad_parts(rows_s, down_cols, r_up, r_act, r_slope)
    grad_gate = contract_rows(rows_x, r_gate).astype(jnp.bfloat16)[None]
    grad_up = contract_rows(rows_x, r_upg).astype(jnp.bfloat16)[None]
    grad_down_t = contract_rows(rows_s, r_hidden).astype(jnp.bfloat16)[None]
    return (mixed, input_grad, grad_gate, grad_up, grad_down_t)


def solution(mesh):
    rows = P(("dp", "expert", "tensor"), None)
    weights = P("expert", ("dp", "tensor"))
    grads = P("expert", None, ("dp", "tensor"))
    return jax.shard_map(
        shards,
        mesh=mesh,
        in_specs=(rows, rows, rows, rows, weights, weights, weights),
        out_specs=(rows, rows, grads, grads, grads),
        check_vma=False,
    )
```

```python
import jax
import jax.numpy as jnp
from jax import lax
from jax.sharding import PartitionSpec as P

GROUP = ("dp", "tensor")


def silu_parts(gate_pre):
    sigmoid_val = jax.nn.sigmoid(gate_pre)
    return (gate_pre * sigmoid_val, sigmoid_val * (1.0 + gate_pre * (1.0 - sigmoid_val)))


def contract_rows(left_side, right_side):
    return lax.dot_general(
        left_side, right_side, (((0,), (0,)), ((), ())), preferred_element_type=jnp.float32
    )


def contract_cols(left_side, right_side):
    return lax.dot_general(
        left_side, right_side, (((1,), (1,)), ((), ())), preferred_element_type=jnp.float32
    )


def forward_parts(rows_x, gate_cols, up_cols):
    gate_pre = jnp.dot(rows_x, gate_cols, preferred_element_type=jnp.float32)
    up_pre = jnp.dot(rows_x, up_cols, preferred_element_type=jnp.float32)
    activation, act_slope = silu_parts(gate_pre)
    hidden = (activation * up_pre).astype(jnp.bfloat16)
    return up_pre, activation, act_slope, hidden


def grad_parts(scaled, down_cols, up_pre, activation, act_slope):
    hidden_grad = jnp.dot(scaled, down_cols, preferred_element_type=jnp.float32)
    gate_grad = (hidden_grad * up_pre * act_slope).astype(jnp.bfloat16)
    up_grad = (hidden_grad * activation).astype(jnp.bfloat16)
    return gate_grad, up_grad


def shards(tokens, cotangent, routes, weight_codes, dense_gate, dense_up, dense_down_t):
    experts = lax.axis_size("expert")
    count_tok, model_width = tokens.shape
    hid = dense_gate.shape[1]
    capacity = 5 * count_tok // (2 * experts)
    slots_here = experts * capacity

    flat_route = routes.reshape(-1)
    flat_scale = weight_codes.reshape(-1).astype(jnp.float32) / 256.0
    onehot = (flat_route[:, None] == jnp.arange(experts, dtype=jnp.int32)[None, :]).astype(
        jnp.int32
    )
    earlier = jnp.cumsum(onehot, axis=0) - onehot
    slot_of = flat_route * capacity + jnp.sum(earlier * onehot, axis=1)
    placed = (slot_of[None, :] == jnp.arange(slots_here, dtype=jnp.int32)[:, None]).astype(
        jnp.bfloat16
    )
    flat_x = jnp.repeat(tokens, 2, axis=0)
    flat_scaled = (flat_scale[:, None] * jnp.repeat(cotangent, 2, axis=0).astype(jnp.float32)).astype(
        jnp.bfloat16
    )
    send_x = jnp.dot(placed, flat_x, preferred_element_type=jnp.float32).astype(jnp.bfloat16)
    send_s = jnp.dot(placed, flat_scaled, preferred_element_type=jnp.float32).astype(jnp.bfloat16)
    send = jnp.concatenate([send_x, send_s], axis=1)

    lane = 1024
    stacked = jnp.concatenate([dense_gate, dense_up, dense_down_t], axis=1)
    w_rows = stacked.size // lane
    copies = jnp.broadcast_to(stacked.reshape(1, w_rows, lane), (experts, w_rows, lane))
    routed = send.reshape(experts, -1, lane)
    parcel = jnp.concatenate([copies, routed], axis=1)
    parcel = lax.all_to_all(parcel, "expert", split_axis=0, concat_axis=0, tiled=True)
    full_cols = parcel[:, :w_rows].reshape(-1, stacked.shape[1])
    got = parcel[:, w_rows:].reshape(slots_here, 2 * model_width)
    gate_cols = full_cols[:, :hid]
    up_cols = full_cols[:, hid : 2 * hid]
    down_cols = full_cols[:, 2 * hid :]
    gate_up_cols = full_cols[:, : 2 * hid]
    code_cols = jnp.zeros((count_tok, 128), jnp.bfloat16)
    code_cols = code_cols.at[:, 0:2].set(weight_codes.astype(jnp.bfloat16))
    home = jnp.concatenate([tokens, cotangent, code_cols], axis=1)
    plane = lax.all_gather(home, GROUP, axis=0, tiled=True)
    plane_x = plane[:, :model_width]
    plane_dy = plane[:, model_width : 2 * model_width].astype(jnp.float32)
    plane_scale = plane[:, 2 * model_width : 2 * model_width + 2].astype(jnp.float32) / 256.0

    up_pre, activation, act_slope, hidden = forward_parts(plane_x, gate_cols, up_cols)
    out_term = contract_cols(hidden, down_cols).astype(jnp.bfloat16)
    grad_term = jnp.zeros(out_term.shape, jnp.float32)
    for which in range(2):
        scaled = (plane_scale[:, which : which + 1] * plane_dy).astype(jnp.bfloat16)
        gate_grad, up_grad = grad_parts(scaled, down_cols, up_pre, activation, act_slope)
        grad_term = grad_term + contract_cols(
            jnp.concatenate([gate_grad, up_grad], axis=1), gate_up_cols
        )
    terms = jnp.concatenate([out_term, grad_term.astype(jnp.bfloat16)], axis=1)

    rows = lax.all_gather(got, GROUP, axis=0, tiled=True)
    n_group = terms.shape[0] // count_tok
    pieces = terms.reshape(n_group, count_tok, 2 * model_width)
    pieces = lax.all_to_all(pieces, GROUP, split_axis=0, concat_axis=0, tiled=True)
    rows_x = rows[:, :model_width]
    rows_s = rows[:, model_width:]
    r_up, r_act, r_slope, r_hidden = forward_parts(rows_x, gate_cols, up_cols)
    r_gate, r_upg = grad_parts(rows_s, down_cols, r_up, r_act, r_slope)
    grad_gate = contract_rows(rows_x, r_gate).astype(jnp.bfloat16)[None]
    grad_up = contract_rows(rows_x, r_upg).astype(jnp.bfloat16)[None]
    grad_down_t = contract_rows(rows_s, r_hidden).astype(jnp.bfloat16)[None]
    pieces, grad_gate, grad_up, grad_down_t = lax.optimization_barrier(
        (pieces, grad_gate, grad_up, grad_down_t)
    )
    summed = jnp.sum(pieces.astype(jnp.float32), axis=0)
    expert_out = summed[:, :model_width].astype(jnp.bfloat16).astype(jnp.float32)
    code_scale = weight_codes.astype(jnp.float32) / 256.0
    mixed = (code_scale[:, 0:1] * expert_out + code_scale[:, 1:2] * expert_out).astype(
        jnp.bfloat16
    )
    input_grad = summed[:, model_width:].astype(jnp.bfloat16)
    return (mixed, input_grad, grad_gate, grad_up, grad_down_t)


def solution(mesh):
    rows = P(("dp", "expert", "tensor"), None)
    weights = P("expert", ("dp", "tensor"))
    grads = P("expert", None, ("dp", "tensor"))
    return jax.shard_map(
        shards,
        mesh=mesh,
        in_specs=(rows, rows, rows, rows, weights, weights, weights),
        out_specs=(rows, rows, grads, grads, grads),
        check_vma=False,
    )
```

```python
import jax
import jax.numpy as jnp
from jax import lax
from jax.sharding import PartitionSpec as P

GROUP = ("dp", "tensor")


def silu_parts(gate_pre):
    sigmoid_val = jax.nn.sigmoid(gate_pre)
    return (gate_pre * sigmoid_val, sigmoid_val * (1.0 + gate_pre * (1.0 - sigmoid_val)))


def contract_rows(left_side, right_side):
    return lax.dot_general(
        left_side, right_side, (((0,), (0,)), ((), ())), preferred_element_type=jnp.float32
    )


def contract_cols(left_side, right_side):
    return lax.dot_general(
        left_side, right_side, (((1,), (1,)), ((), ())), preferred_element_type=jnp.float32
    )


def forward_parts(rows_x, gate_cols, up_cols):
    gate_pre = jnp.dot(rows_x, gate_cols, preferred_element_type=jnp.float32)
    up_pre = jnp.dot(rows_x, up_cols, preferred_element_type=jnp.float32)
    activation, act_slope = silu_parts(gate_pre)
    hidden = (activation * up_pre).astype(jnp.bfloat16)
    return up_pre, activation, act_slope, hidden


def grad_parts(scaled, down_cols, up_pre, activation, act_slope):
    hidden_grad = jnp.dot(scaled, down_cols, preferred_element_type=jnp.float32)
    gate_grad = (hidden_grad * up_pre * act_slope).astype(jnp.bfloat16)
    up_grad = (hidden_grad * activation).astype(jnp.bfloat16)
    return gate_grad, up_grad


def shards(tokens, cotangent, routes, weight_codes, dense_gate, dense_up, dense_down_t):
    experts = lax.axis_size("expert")
    count_tok, model_width = tokens.shape
    hid = dense_gate.shape[1]
    capacity = 5 * count_tok // (2 * experts)
    slots_here = experts * capacity

    stacked = jnp.concatenate([dense_gate, dense_up, dense_down_t], axis=1)
    copies = jnp.broadcast_to(stacked[None], (experts,) + stacked.shape)
    full_cols = lax.all_to_all(copies, "expert", split_axis=0, concat_axis=0, tiled=True)
    full_cols = full_cols.reshape(-1, stacked.shape[1])
    gate_cols = full_cols[:, :hid]
    up_cols = full_cols[:, hid : 2 * hid]
    down_cols = full_cols[:, 2 * hid :]
    gate_up_cols = full_cols[:, : 2 * hid]

    code_cols = jnp.zeros((count_tok, 128), jnp.bfloat16)
    code_cols = code_cols.at[:, 0:2].set(weight_codes.astype(jnp.bfloat16))
    home = jnp.concatenate([tokens, cotangent, code_cols], axis=1)
    plane = lax.all_gather(home, GROUP, axis=0, tiled=True)
    plane_x = plane[:, :model_width]
    plane_dy = plane[:, model_width : 2 * model_width].astype(jnp.float32)
    plane_scale = plane[:, 2 * model_width : 2 * model_width + 2].astype(jnp.float32) / 256.0

    up_pre, activation, act_slope, hidden = forward_parts(plane_x, gate_cols, up_cols)
    out_term = contract_cols(hidden, down_cols).astype(jnp.bfloat16)
    grad_term = jnp.zeros(out_term.shape, jnp.float32)
    for which in range(2):
        scaled = (plane_scale[:, which : which + 1] * plane_dy).astype(jnp.bfloat16)
        gate_grad, up_grad = grad_parts(scaled, down_cols, up_pre, activation, act_slope)
        grad_term = grad_term + contract_cols(
            jnp.concatenate([gate_grad, up_grad], axis=1), gate_up_cols
        )
    terms = jnp.concatenate([out_term, grad_term.astype(jnp.bfloat16)], axis=1)

    flat_route = routes.reshape(-1)
    flat_scale = weight_codes.reshape(-1).astype(jnp.float32) / 256.0
    onehot = (flat_route[:, None] == jnp.arange(experts, dtype=jnp.int32)[None, :]).astype(
        jnp.int32
    )
    earlier = jnp.cumsum(onehot, axis=0) - onehot
    slot_of = flat_route * capacity + jnp.sum(earlier * onehot, axis=1)
    placed = (slot_of[None, :] == jnp.arange(slots_here, dtype=jnp.int32)[:, None]).astype(
        jnp.bfloat16
    )
    flat_x = jnp.repeat(tokens, 2, axis=0)
    flat_scaled = (flat_scale[:, None] * jnp.repeat(cotangent, 2, axis=0).astype(jnp.float32)).astype(
        jnp.bfloat16
    )
    send_x = jnp.dot(placed, flat_x, preferred_element_type=jnp.float32).astype(jnp.bfloat16)
    send_s = jnp.dot(placed, flat_scaled, preferred_element_type=jnp.float32).astype(jnp.bfloat16)
    send = jnp.concatenate([send_x, send_s], axis=1)
    got = lax.all_to_all(send, "expert", split_axis=0, concat_axis=0, tiled=True)
    rows = lax.all_gather(got, GROUP, axis=0, tiled=True)
    n_group = terms.shape[0] // count_tok
    pieces = terms.reshape(n_group, count_tok, 2 * model_width)
    pieces = lax.all_to_all(pieces, GROUP, split_axis=0, concat_axis=0, tiled=True)
    rows_x = rows[:, :model_width]
    rows_s = rows[:, model_width:]
    r_up, r_act, r_slope, r_hidden = forward_parts(rows_x, gate_cols, up_cols)
    r_gate, r_upg = grad_parts(rows_s, down_cols, r_up, r_act, r_slope)
    grad_gate = contract_rows(rows_x, r_gate).astype(jnp.bfloat16)[None]
    grad_up = contract_rows(rows_x, r_upg).astype(jnp.bfloat16)[None]
    grad_down_t = contract_rows(rows_s, r_hidden).astype(jnp.bfloat16)[None]
    pieces, grad_gate, grad_up, grad_down_t = lax.optimization_barrier(
        (pieces, grad_gate, grad_up, grad_down_t)
    )
    summed = jnp.sum(pieces.astype(jnp.float32), axis=0)
    expert_out = summed[:, :model_width].astype(jnp.bfloat16).astype(jnp.float32)
    code_scale = weight_codes.astype(jnp.float32) / 256.0
    mixed = (code_scale[:, 0:1] * expert_out + code_scale[:, 1:2] * expert_out).astype(
        jnp.bfloat16
    )
    input_grad = summed[:, model_width:].astype(jnp.bfloat16)
    return (mixed, input_grad, grad_gate, grad_up, grad_down_t)


def solution(mesh):
    rows = P(("dp", "expert", "tensor"), None)
    weights = P("expert", ("dp", "tensor"))
    grads = P("expert", None, ("dp", "tensor"))
    return jax.shard_map(
        shards,
        mesh=mesh,
        in_specs=(rows, rows, rows, rows, weights, weights, weights),
        out_specs=(rows, rows, grads, grads, grads),
        check_vma=False,
    )
```

```python
import jax
import jax.numpy as jnp
from jax import lax
from jax.sharding import PartitionSpec as P

GROUP = ("dp", "tensor")


def silu_parts(gate_pre):
    sigmoid_val = jax.nn.sigmoid(gate_pre)
    return (gate_pre * sigmoid_val, sigmoid_val * (1.0 + gate_pre * (1.0 - sigmoid_val)))


def contract_rows(left_side, right_side):
    return lax.dot_general(
        left_side, right_side, (((0,), (0,)), ((), ())), preferred_element_type=jnp.float32
    )


def contract_cols(left_side, right_side):
    return lax.dot_general(
        left_side, right_side, (((1,), (1,)), ((), ())), preferred_element_type=jnp.float32
    )


def forward_parts(rows_x, gate_cols, up_cols):
    gate_pre = jnp.dot(rows_x, gate_cols, preferred_element_type=jnp.float32)
    up_pre = jnp.dot(rows_x, up_cols, preferred_element_type=jnp.float32)
    activation, act_slope = silu_parts(gate_pre)
    hidden = (activation * up_pre).astype(jnp.bfloat16)
    return up_pre, activation, act_slope, hidden


def grad_parts(scaled, down_cols, up_pre, activation, act_slope):
    hidden_grad = jnp.dot(scaled, down_cols, preferred_element_type=jnp.float32)
    gate_grad = (hidden_grad * up_pre * act_slope).astype(jnp.bfloat16)
    up_grad = (hidden_grad * activation).astype(jnp.bfloat16)
    return gate_grad, up_grad


def shards(tokens, cotangent, routes, weight_codes, dense_gate, dense_up, dense_down_t):
    experts = lax.axis_size("expert")
    count_tok, model_width = tokens.shape
    hid = dense_gate.shape[1]
    capacity = 5 * count_tok // (2 * experts)
    slots_here = experts * capacity

    stacked = jnp.concatenate([dense_gate, dense_up, dense_down_t], axis=1)
    copies = jnp.broadcast_to(stacked[None], (experts,) + stacked.shape)
    full_cols = lax.all_to_all(copies, "expert", split_axis=0, concat_axis=0, tiled=True)
    full_cols = full_cols.reshape(-1, stacked.shape[1])
    gate_cols = full_cols[:, :hid]
    up_cols = full_cols[:, hid : 2 * hid]
    down_cols = full_cols[:, 2 * hid :]
    gate_up_cols = full_cols[:, : 2 * hid]

    code_cols = jnp.zeros((count_tok, 128), jnp.bfloat16)
    code_cols = code_cols.at[:, 0:2].set(weight_codes.astype(jnp.bfloat16))
    home = jnp.concatenate([tokens, cotangent, code_cols], axis=1)
    plane = lax.all_gather(home, GROUP, axis=0, tiled=True)
    plane_x = plane[:, :model_width]
    plane_dy = plane[:, model_width : 2 * model_width].astype(jnp.float32)
    plane_scale = plane[:, 2 * model_width : 2 * model_width + 2].astype(jnp.float32) / 256.0

    up_pre, activation, act_slope, hidden = forward_parts(plane_x, gate_cols, up_cols)
    out_term = contract_cols(hidden, down_cols).astype(jnp.bfloat16)
    grad_term = jnp.zeros(out_term.shape, jnp.float32)
    for which in range(2):
        scaled = (plane_scale[:, which : which + 1] * plane_dy).astype(jnp.bfloat16)
        gate_grad, up_grad = grad_parts(scaled, down_cols, up_pre, activation, act_slope)
        grad_term = grad_term + contract_cols(
            jnp.concatenate([gate_grad, up_grad], axis=1), gate_up_cols
        )
    terms = jnp.concatenate([out_term, grad_term.astype(jnp.bfloat16)], axis=1)

    flat_route = routes.reshape(-1)
    flat_scale = weight_codes.reshape(-1).astype(jnp.float32) / 256.0
    onehot = (flat_route[:, None] == jnp.arange(experts, dtype=jnp.int32)[None, :]).astype(
        jnp.int32
    )
    earlier = jnp.cumsum(onehot, axis=0) - onehot
    slot_of = flat_route * capacity + jnp.sum(earlier * onehot, axis=1)
    placed = (slot_of[None, :] == jnp.arange(slots_here, dtype=jnp.int32)[:, None]).astype(
        jnp.bfloat16
    )
    flat_x = jnp.repeat(tokens, 2, axis=0)
    flat_scaled = (flat_scale[:, None] * jnp.repeat(cotangent, 2, axis=0).astype(jnp.float32)).astype(
        jnp.bfloat16
    )
    send_x = jnp.dot(placed, flat_x, preferred_element_type=jnp.float32).astype(jnp.bfloat16)
    send_s = jnp.dot(placed, flat_scaled, preferred_element_type=jnp.float32).astype(jnp.bfloat16)
    send = jnp.concatenate([send_x, send_s], axis=1)
    got = lax.all_to_all(send, "expert", split_axis=0, concat_axis=0, tiled=True)
    rows = lax.all_gather(got, GROUP, axis=0, tiled=True)
    n_dp = lax.axis_size("dp")
    n_tensor = lax.axis_size("tensor")
    pieces = terms.reshape(n_dp, n_tensor, count_tok, 2 * model_width)
    pieces = lax.all_to_all(pieces, "tensor", split_axis=1, concat_axis=1, tiled=True)
    pieces = jnp.sum(pieces.astype(jnp.float32), axis=1).astype(jnp.bfloat16)
    pieces = lax.all_to_all(pieces, "dp", split_axis=0, concat_axis=0, tiled=True)
    rows_x = rows[:, :model_width]
    rows_s = rows[:, model_width:]
    r_up, r_act, r_slope, r_hidden = forward_parts(rows_x, gate_cols, up_cols)
    r_gate, r_upg = grad_parts(rows_s, down_cols, r_up, r_act, r_slope)
    grad_gate = contract_rows(rows_x, r_gate).astype(jnp.bfloat16)[None]
    grad_up = contract_rows(rows_x, r_upg).astype(jnp.bfloat16)[None]
    grad_down_t = contract_rows(rows_s, r_hidden).astype(jnp.bfloat16)[None]
    pieces, grad_gate, grad_up, grad_down_t = lax.optimization_barrier(
        (pieces, grad_gate, grad_up, grad_down_t)
    )
    summed = jnp.sum(pieces.astype(jnp.float32), axis=0)
    expert_out = summed[:, :model_width].astype(jnp.bfloat16).astype(jnp.float32)
    code_scale = weight_codes.astype(jnp.float32) / 256.0
    mixed = (code_scale[:, 0:1] * expert_out + code_scale[:, 1:2] * expert_out).astype(
        jnp.bfloat16
    )
    input_grad = summed[:, model_width:].astype(jnp.bfloat16)
    return (mixed, input_grad, grad_gate, grad_up, grad_down_t)


def solution(mesh):
    rows = P(("dp", "expert", "tensor"), None)
    weights = P("expert", ("dp", "tensor"))
    grads = P("expert", None, ("dp", "tensor"))
    return jax.shard_map(
        shards,
        mesh=mesh,
        in_specs=(rows, rows, rows, rows, weights, weights, weights),
        out_specs=(rows, rows, grads, grads, grads),
        check_vma=False,
    )
```

```python
import jax
import jax.numpy as jnp
from jax import lax
from jax.sharding import PartitionSpec as P

GROUP = ("dp", "tensor")


def silu_parts(gate_pre):
    sigmoid_val = jax.nn.sigmoid(gate_pre)
    return (gate_pre * sigmoid_val, sigmoid_val * (1.0 + gate_pre * (1.0 - sigmoid_val)))


def contract_rows(left_side, right_side):
    return lax.dot_general(
        left_side, right_side, (((0,), (0,)), ((), ())), preferred_element_type=jnp.float32
    )


def contract_cols(left_side, right_side):
    return lax.dot_general(
        left_side, right_side, (((1,), (1,)), ((), ())), preferred_element_type=jnp.float32
    )


def forward_parts(rows_x, gate_cols, up_cols):
    gate_pre = jnp.dot(rows_x, gate_cols, preferred_element_type=jnp.float32)
    up_pre = jnp.dot(rows_x, up_cols, preferred_element_type=jnp.float32)
    activation, act_slope = silu_parts(gate_pre)
    hidden = (activation * up_pre).astype(jnp.bfloat16)
    return up_pre, activation, act_slope, hidden


def grad_parts(scaled, down_cols, up_pre, activation, act_slope):
    hidden_grad = jnp.dot(scaled, down_cols, preferred_element_type=jnp.float32)
    gate_grad = (hidden_grad * up_pre * act_slope).astype(jnp.bfloat16)
    up_grad = (hidden_grad * activation).astype(jnp.bfloat16)
    return gate_grad, up_grad


def shards(tokens, cotangent, routes, weight_codes, dense_gate, dense_up, dense_down_t):
    experts = lax.axis_size("expert")
    count_tok, model_width = tokens.shape
    hid = dense_gate.shape[1]
    capacity = 5 * count_tok // (2 * experts)
    slots_here = experts * capacity

    stacked = jnp.concatenate([dense_gate, dense_up, dense_down_t], axis=1)
    copies = jnp.broadcast_to(stacked[None], (experts,) + stacked.shape)
    full_cols = lax.all_to_all(copies, "expert", split_axis=0, concat_axis=0, tiled=True)
    full_cols = full_cols.reshape(-1, stacked.shape[1])
    gate_cols = full_cols[:, :hid]
    up_cols = full_cols[:, hid : 2 * hid]
    down_cols = full_cols[:, 2 * hid :]
    gate_up_cols = full_cols[:, : 2 * hid]

    code_cols = jnp.zeros((count_tok, 128), jnp.bfloat16)
    code_cols = code_cols.at[:, 0:2].set(weight_codes.astype(jnp.bfloat16))
    home = jnp.concatenate([tokens, cotangent, code_cols], axis=1)
    plane = lax.all_gather(home, "tensor", axis=0, tiled=True)
    plane = lax.all_gather(plane, "dp", axis=0, tiled=True)
    plane_x = plane[:, :model_width]
    plane_dy = plane[:, model_width : 2 * model_width].astype(jnp.float32)
    plane_scale = plane[:, 2 * model_width : 2 * model_width + 2].astype(jnp.float32) / 256.0

    up_pre, activation, act_slope, hidden = forward_parts(plane_x, gate_cols, up_cols)
    out_term = contract_cols(hidden, down_cols).astype(jnp.bfloat16)
    grad_term = jnp.zeros(out_term.shape, jnp.float32)
    for which in range(2):
        scaled = (plane_scale[:, which : which + 1] * plane_dy).astype(jnp.bfloat16)
        gate_grad, up_grad = grad_parts(scaled, down_cols, up_pre, activation, act_slope)
        grad_term = grad_term + contract_cols(
            jnp.concatenate([gate_grad, up_grad], axis=1), gate_up_cols
        )
    terms = jnp.concatenate([out_term, grad_term.astype(jnp.bfloat16)], axis=1)

    flat_route = routes.reshape(-1)
    flat_scale = weight_codes.reshape(-1).astype(jnp.float32) / 256.0
    onehot = (flat_route[:, None] == jnp.arange(experts, dtype=jnp.int32)[None, :]).astype(
        jnp.int32
    )
    earlier = jnp.cumsum(onehot, axis=0) - onehot
    slot_of = flat_route * capacity + jnp.sum(earlier * onehot, axis=1)
    placed = (slot_of[None, :] == jnp.arange(slots_here, dtype=jnp.int32)[:, None]).astype(
        jnp.bfloat16
    )
    flat_x = jnp.repeat(tokens, 2, axis=0)
    flat_scaled = (flat_scale[:, None] * jnp.repeat(cotangent, 2, axis=0).astype(jnp.float32)).astype(
        jnp.bfloat16
    )
    send_x = jnp.dot(placed, flat_x, preferred_element_type=jnp.float32).astype(jnp.bfloat16)
    send_s = jnp.dot(placed, flat_scaled, preferred_element_type=jnp.float32).astype(jnp.bfloat16)
    send = jnp.concatenate([send_x, send_s], axis=1)
    got = lax.all_to_all(send, "expert", split_axis=0, concat_axis=0, tiled=True)
    rows = lax.all_gather(got, GROUP, axis=0, tiled=True)
    n_group = terms.shape[0] // count_tok
    pieces = terms.reshape(n_group, count_tok, 2 * model_width)
    pieces = lax.all_to_all(pieces, GROUP, split_axis=0, concat_axis=0, tiled=True)
    rows_x = rows[:, :model_width]
    rows_s = rows[:, model_width:]
    r_up, r_act, r_slope, r_hidden = forward_parts(rows_x, gate_cols, up_cols)
    r_gate, r_upg = grad_parts(rows_s, down_cols, r_up, r_act, r_slope)
    grad_gate = contract_rows(rows_x, r_gate).astype(jnp.bfloat16)[None]
    grad_up = contract_rows(rows_x, r_upg).astype(jnp.bfloat16)[None]
    grad_down_t = contract_rows(rows_s, r_hidden).astype(jnp.bfloat16)[None]
    pieces, grad_gate, grad_up, grad_down_t = lax.optimization_barrier(
        (pieces, grad_gate, grad_up, grad_down_t)
    )
    summed = jnp.sum(pieces.astype(jnp.float32), axis=0)
    expert_out = summed[:, :model_width].astype(jnp.bfloat16).astype(jnp.float32)
    code_scale = weight_codes.astype(jnp.float32) / 256.0
    mixed = (code_scale[:, 0:1] * expert_out + code_scale[:, 1:2] * expert_out).astype(
        jnp.bfloat16
    )
    input_grad = summed[:, model_width:].astype(jnp.bfloat16)
    return (mixed, input_grad, grad_gate, grad_up, grad_down_t)


def solution(mesh):
    rows = P(("dp", "expert", "tensor"), None)
    weights = P("expert", ("dp", "tensor"))
    grads = P("expert", None, ("dp", "tensor"))
    return jax.shard_map(
        shards,
        mesh=mesh,
        in_specs=(rows, rows, rows, rows, weights, weights, weights),
        out_specs=(rows, rows, grads, grads, grads),
        check_vma=False,
    )
```

```python
import jax
import jax.numpy as jnp
from jax import lax
from jax.sharding import PartitionSpec as P

GROUP = ("dp", "tensor")


def silu_parts(gate_pre):
    sigmoid_val = jax.nn.sigmoid(gate_pre)
    return (gate_pre * sigmoid_val, sigmoid_val * (1.0 + gate_pre * (1.0 - sigmoid_val)))


def contract_rows(left_side, right_side):
    return lax.dot_general(
        left_side, right_side, (((0,), (0,)), ((), ())), preferred_element_type=jnp.float32
    )


def contract_cols(left_side, right_side):
    return lax.dot_general(
        left_side, right_side, (((1,), (1,)), ((), ())), preferred_element_type=jnp.float32
    )


def forward_parts(rows_x, gate_cols, up_cols):
    gate_pre = jnp.dot(rows_x, gate_cols, preferred_element_type=jnp.float32)
    up_pre = jnp.dot(rows_x, up_cols, preferred_element_type=jnp.float32)
    activation, act_slope = silu_parts(gate_pre)
    hidden = (activation * up_pre).astype(jnp.bfloat16)
    return up_pre, activation, act_slope, hidden


def grad_parts(scaled, down_cols, up_pre, activation, act_slope):
    hidden_grad = jnp.dot(scaled, down_cols, preferred_element_type=jnp.float32)
    gate_grad = (hidden_grad * up_pre * act_slope).astype(jnp.bfloat16)
    up_grad = (hidden_grad * activation).astype(jnp.bfloat16)
    return gate_grad, up_grad


def shards(tokens, cotangent, routes, weight_codes, dense_gate, dense_up, dense_down_t):
    experts = lax.axis_size("expert")
    count_tok, model_width = tokens.shape
    hid = dense_gate.shape[1]
    capacity = 5 * count_tok // (2 * experts)
    slots_here = experts * capacity

    stacked = jnp.concatenate([dense_gate, dense_up, dense_down_t], axis=1)
    copies = jnp.broadcast_to(stacked[None], (experts,) + stacked.shape)
    full_cols = lax.all_to_all(copies, "expert", split_axis=0, concat_axis=0, tiled=True)
    full_cols = full_cols.reshape(-1, stacked.shape[1])
    gate_cols = full_cols[:, :hid]
    up_cols = full_cols[:, hid : 2 * hid]
    down_cols = full_cols[:, 2 * hid :]
    gate_up_cols = full_cols[:, : 2 * hid]

    code_cols = jnp.zeros((count_tok, 128), jnp.bfloat16)
    code_cols = code_cols.at[:, 0:2].set(weight_codes.astype(jnp.bfloat16))
    home = jnp.concatenate([tokens, cotangent, code_cols], axis=1)
    plane = lax.all_gather(home, GROUP, axis=0, tiled=True)
    plane_x = plane[:, :model_width]
    plane_dy = plane[:, model_width : 2 * model_width].astype(jnp.float32)
    plane_scale = plane[:, 2 * model_width : 2 * model_width + 2].astype(jnp.float32) / 256.0

    up_pre, activation, act_slope, hidden = forward_parts(plane_x, gate_cols, up_cols)
    out_term = contract_cols(hidden, down_cols).astype(jnp.bfloat16)
    grad_term = jnp.zeros(out_term.shape, jnp.float32)
    for which in range(2):
        scaled = (plane_scale[:, which : which + 1] * plane_dy).astype(jnp.bfloat16)
        gate_grad, up_grad = grad_parts(scaled, down_cols, up_pre, activation, act_slope)
        grad_term = grad_term + contract_cols(
            jnp.concatenate([gate_grad, up_grad], axis=1), gate_up_cols
        )

    flat_route = routes.reshape(-1)
    flat_scale = weight_codes.reshape(-1).astype(jnp.float32) / 256.0
    onehot = (flat_route[:, None] == jnp.arange(experts, dtype=jnp.int32)[None, :]).astype(
        jnp.int32
    )
    earlier = jnp.cumsum(onehot, axis=0) - onehot
    slot_of = flat_route * capacity + jnp.sum(earlier * onehot, axis=1)
    placed = (slot_of[None, :] == jnp.arange(slots_here, dtype=jnp.int32)[:, None]).astype(
        jnp.bfloat16
    )
    flat_x = jnp.repeat(tokens, 2, axis=0)
    flat_scaled = (flat_scale[:, None] * jnp.repeat(cotangent, 2, axis=0).astype(jnp.float32)).astype(
        jnp.bfloat16
    )
    send_x = jnp.dot(placed, flat_x, preferred_element_type=jnp.float32).astype(jnp.bfloat16)
    send_s = jnp.dot(placed, flat_scaled, preferred_element_type=jnp.float32).astype(jnp.bfloat16)
    send = jnp.concatenate([send_x, send_s], axis=1)
    got = lax.all_to_all(send, "expert", split_axis=0, concat_axis=0, tiled=True)
    rows = lax.all_gather(got, GROUP, axis=0, tiled=True)
    n_group = out_term.shape[0] // count_tok
    out_pieces = out_term.reshape(n_group, count_tok, model_width)
    out_pieces = lax.all_to_all(out_pieces, GROUP, split_axis=0, concat_axis=0, tiled=True)
    out_pieces, grad_term = lax.optimization_barrier((out_pieces, grad_term))
    grad_pieces = grad_term.astype(jnp.bfloat16).reshape(n_group, count_tok, model_width)
    grad_pieces = lax.all_to_all(grad_pieces, GROUP, split_axis=0, concat_axis=0, tiled=True)
    rows_x = rows[:, :model_width]
    rows_s = rows[:, model_width:]
    r_up, r_act, r_slope, r_hidden = forward_parts(rows_x, gate_cols, up_cols)
    r_gate, r_upg = grad_parts(rows_s, down_cols, r_up, r_act, r_slope)
    grad_gate = contract_rows(rows_x, r_gate).astype(jnp.bfloat16)[None]
    grad_up = contract_rows(rows_x, r_upg).astype(jnp.bfloat16)[None]
    grad_down_t = contract_rows(rows_s, r_hidden).astype(jnp.bfloat16)[None]
    out_pieces, grad_pieces, grad_gate, grad_up, grad_down_t = lax.optimization_barrier(
        (out_pieces, grad_pieces, grad_gate, grad_up, grad_down_t)
    )
    expert_out = jnp.sum(out_pieces.astype(jnp.float32), axis=0)
    expert_out = expert_out.astype(jnp.bfloat16).astype(jnp.float32)
    code_scale = weight_codes.astype(jnp.float32) / 256.0
    mixed = (code_scale[:, 0:1] * expert_out + code_scale[:, 1:2] * expert_out).astype(
        jnp.bfloat16
    )
    input_grad = jnp.sum(grad_pieces.astype(jnp.float32), axis=0).astype(jnp.bfloat16)
    return (mixed, input_grad, grad_gate, grad_up, grad_down_t)


def solution(mesh):
    rows = P(("dp", "expert", "tensor"), None)
    weights = P("expert", ("dp", "tensor"))
    grads = P("expert", None, ("dp", "tensor"))
    return jax.shard_map(
        shards,
        mesh=mesh,
        in_specs=(rows, rows, rows, rows, weights, weights, weights),
        out_specs=(rows, rows, grads, grads, grads),
        check_vma=False,
    )
```

```python
import jax
import jax.numpy as jnp
from jax import lax
from jax.sharding import PartitionSpec as P

GROUP = ("dp", "tensor")


def silu_parts(gate_pre):
    sigmoid_val = jax.nn.sigmoid(gate_pre)
    return (gate_pre * sigmoid_val, sigmoid_val * (1.0 + gate_pre * (1.0 - sigmoid_val)))


def contract_rows(left_side, right_side):
    return lax.dot_general(
        left_side, right_side, (((0,), (0,)), ((), ())), preferred_element_type=jnp.float32
    )


def contract_cols(left_side, right_side):
    return lax.dot_general(
        left_side, right_side, (((1,), (1,)), ((), ())), preferred_element_type=jnp.float32
    )


def forward_parts(rows_x, gate_cols, up_cols):
    gate_pre = jnp.dot(rows_x, gate_cols, preferred_element_type=jnp.float32)
    up_pre = jnp.dot(rows_x, up_cols, preferred_element_type=jnp.float32)
    activation, act_slope = silu_parts(gate_pre)
    hidden = (activation * up_pre).astype(jnp.bfloat16)
    return up_pre, activation, act_slope, hidden


def grad_parts(scaled, down_cols, up_pre, activation, act_slope):
    hidden_grad = jnp.dot(scaled, down_cols, preferred_element_type=jnp.float32)
    gate_grad = (hidden_grad * up_pre * act_slope).astype(jnp.bfloat16)
    up_grad = (hidden_grad * activation).astype(jnp.bfloat16)
    return gate_grad, up_grad


def shards(tokens, cotangent, routes, weight_codes, dense_gate, dense_up, dense_down_t):
    experts = lax.axis_size("expert")
    count_tok, model_width = tokens.shape
    hid = dense_gate.shape[1]
    capacity = 5 * count_tok // (2 * experts)
    slots_here = experts * capacity

    stacked = jnp.concatenate([dense_gate, dense_up, dense_down_t], axis=1)
    copies = jnp.broadcast_to(stacked[None], (experts,) + stacked.shape)
    full_cols = lax.all_to_all(copies, "expert", split_axis=0, concat_axis=0, tiled=True)
    full_cols = full_cols.reshape(-1, stacked.shape[1])
    gate_cols = full_cols[:, :hid]
    up_cols = full_cols[:, hid : 2 * hid]
    down_cols = full_cols[:, 2 * hid :]
    gate_up_cols = full_cols[:, : 2 * hid]

    code_cols = jnp.pad(weight_codes.astype(jnp.bfloat16), ((0, 0), (0, 126)))
    home = jnp.concatenate([tokens, cotangent, code_cols], axis=1)
    plane = lax.all_gather(home, GROUP, axis=0, tiled=True)
    plane_x = plane[:, :model_width]
    plane_dy = plane[:, model_width : 2 * model_width].astype(jnp.float32)
    plane_scale = plane[:, 2 * model_width : 2 * model_width + 2].astype(jnp.float32) / 256.0

    up_pre, activation, act_slope, hidden = forward_parts(plane_x, gate_cols, up_cols)
    out_term = contract_cols(hidden, down_cols).astype(jnp.bfloat16)
    grad_term = jnp.zeros(out_term.shape, jnp.float32)
    for which in range(2):
        scaled = (plane_scale[:, which : which + 1] * plane_dy).astype(jnp.bfloat16)
        gate_grad, up_grad = grad_parts(scaled, down_cols, up_pre, activation, act_slope)
        grad_term = grad_term + contract_cols(
            jnp.concatenate([gate_grad, up_grad], axis=1), gate_up_cols
        )
    terms = jnp.concatenate([out_term, grad_term.astype(jnp.bfloat16)], axis=1)

    flat_route = routes.reshape(-1)
    flat_scale = weight_codes.reshape(-1).astype(jnp.float32) / 256.0
    onehot = (flat_route[:, None] == jnp.arange(experts, dtype=jnp.int32)[None, :]).astype(
        jnp.int32
    )
    earlier = jnp.cumsum(onehot, axis=0) - onehot
    slot_of = flat_route * capacity + jnp.sum(earlier * onehot, axis=1)
    placed = (slot_of[None, :] == jnp.arange(slots_here, dtype=jnp.int32)[:, None]).astype(
        jnp.bfloat16
    )
    flat_x = jnp.repeat(tokens, 2, axis=0)
    flat_scaled = (flat_scale[:, None] * jnp.repeat(cotangent, 2, axis=0).astype(jnp.float32)).astype(
        jnp.bfloat16
    )
    send_x = jnp.dot(placed, flat_x, preferred_element_type=jnp.float32).astype(jnp.bfloat16)
    send_s = jnp.dot(placed, flat_scaled, preferred_element_type=jnp.float32).astype(jnp.bfloat16)
    send = jnp.concatenate([send_x, send_s], axis=1)
    got = lax.all_to_all(send, "expert", split_axis=0, concat_axis=0, tiled=True)
    rows = lax.all_gather(got, GROUP, axis=0, tiled=True)
    n_group = terms.shape[0] // count_tok
    pieces = terms.reshape(n_group, count_tok, 2 * model_width)
    pieces = lax.all_to_all(pieces, GROUP, split_axis=0, concat_axis=0, tiled=True)
    rows_x = rows[:, :model_width]
    rows_s = rows[:, model_width:]
    r_up, r_act, r_slope, r_hidden = forward_parts(rows_x, gate_cols, up_cols)
    r_gate, r_upg = grad_parts(rows_s, down_cols, r_up, r_act, r_slope)
    grad_gate = contract_rows(rows_x, r_gate).astype(jnp.bfloat16)[None]
    grad_up = contract_rows(rows_x, r_upg).astype(jnp.bfloat16)[None]
    grad_down_t = contract_rows(rows_s, r_hidden).astype(jnp.bfloat16)[None]
    pieces, grad_gate, grad_up, grad_down_t = lax.optimization_barrier(
        (pieces, grad_gate, grad_up, grad_down_t)
    )
    summed = jnp.sum(pieces.astype(jnp.float32), axis=0)
    expert_out = summed[:, :model_width].astype(jnp.bfloat16).astype(jnp.float32)
    code_scale = weight_codes.astype(jnp.float32) / 256.0
    mixed = (code_scale[:, 0:1] * expert_out + code_scale[:, 1:2] * expert_out).astype(
        jnp.bfloat16
    )
    input_grad = summed[:, model_width:].astype(jnp.bfloat16)
    return (mixed, input_grad, grad_gate, grad_up, grad_down_t)


def solution(mesh):
    rows = P(("dp", "expert", "tensor"), None)
    weights = P("expert", ("dp", "tensor"))
    grads = P("expert", None, ("dp", "tensor"))
    return jax.shard_map(
        shards,
        mesh=mesh,
        in_specs=(rows, rows, rows, rows, weights, weights, weights),
        out_specs=(rows, rows, grads, grads, grads),
        check_vma=False,
    )
```

```python
import jax
import jax.numpy as jnp
from jax import lax
from jax.sharding import PartitionSpec as P

GROUP = ("dp", "tensor")


def silu_parts(gate_pre):
    sigmoid_val = jax.nn.sigmoid(gate_pre)
    return (gate_pre * sigmoid_val, sigmoid_val * (1.0 + gate_pre * (1.0 - sigmoid_val)))


def contract_rows(left_side, right_side):
    return lax.dot_general(
        left_side, right_side, (((0,), (0,)), ((), ())), preferred_element_type=jnp.float32
    )


def contract_cols(left_side, right_side):
    return lax.dot_general(
        left_side, right_side, (((1,), (1,)), ((), ())), preferred_element_type=jnp.float32
    )


def forward_parts(rows_x, gate_cols, up_cols):
    gate_pre = jnp.dot(rows_x, gate_cols, preferred_element_type=jnp.float32)
    up_pre = jnp.dot(rows_x, up_cols, preferred_element_type=jnp.float32)
    activation, act_slope = silu_parts(gate_pre)
    hidden = (activation * up_pre).astype(jnp.bfloat16)
    return up_pre, activation, act_slope, hidden


def grad_parts(scaled, down_cols, up_pre, activation, act_slope):
    hidden_grad = jnp.dot(scaled, down_cols, preferred_element_type=jnp.float32)
    gate_grad = (hidden_grad * up_pre * act_slope).astype(jnp.bfloat16)
    up_grad = (hidden_grad * activation).astype(jnp.bfloat16)
    return gate_grad, up_grad


def shards(tokens, cotangent, routes, weight_codes, dense_gate, dense_up, dense_down_t):
    experts = lax.axis_size("expert")
    count_tok, model_width = tokens.shape
    hid = dense_gate.shape[1]
    capacity = 5 * count_tok // (2 * experts)
    slots_here = experts * capacity

    stacked = jnp.concatenate([dense_gate, dense_up, dense_down_t], axis=1)
    copies = jnp.broadcast_to(stacked[None], (experts,) + stacked.shape)
    full_cols = lax.all_to_all(copies, "expert", split_axis=0, concat_axis=0, tiled=True)
    full_cols = full_cols.reshape(-1, stacked.shape[1])
    gate_cols = full_cols[:, :hid]
    up_cols = full_cols[:, hid : 2 * hid]
    down_cols = full_cols[:, 2 * hid :]
    gate_up_cols = full_cols[:, : 2 * hid]

    code_scale = weight_codes.astype(jnp.float32) / 256.0
    pair_scale = code_scale[:, 0:1] + code_scale[:, 1:2]
    pair_scaled = (pair_scale * cotangent.astype(jnp.float32)).astype(jnp.bfloat16)
    home = jnp.concatenate([tokens, pair_scaled], axis=1)
    plane = lax.all_gather(home, GROUP, axis=0, tiled=True)
    plane_x = plane[:, :model_width]
    plane_s = plane[:, model_width:]

    up_pre, activation, act_slope, hidden = forward_parts(plane_x, gate_cols, up_cols)
    out_term = contract_cols(hidden, down_cols).astype(jnp.bfloat16)
    gate_grad, up_grad = grad_parts(plane_s, down_cols, up_pre, activation, act_slope)
    grad_term = contract_cols(jnp.concatenate([gate_grad, up_grad], axis=1), gate_up_cols)
    terms = jnp.concatenate([out_term, grad_term.astype(jnp.bfloat16)], axis=1)

    flat_route = routes.reshape(-1)
    flat_scale = weight_codes.reshape(-1).astype(jnp.float32) / 256.0
    onehot = (flat_route[:, None] == jnp.arange(experts, dtype=jnp.int32)[None, :]).astype(
        jnp.int32
    )
    earlier = jnp.cumsum(onehot, axis=0) - onehot
    slot_of = flat_route * capacity + jnp.sum(earlier * onehot, axis=1)
    placed = (slot_of[None, :] == jnp.arange(slots_here, dtype=jnp.int32)[:, None]).astype(
        jnp.bfloat16
    )
    flat_x = jnp.repeat(tokens, 2, axis=0)
    flat_scaled = (flat_scale[:, None] * jnp.repeat(cotangent, 2, axis=0).astype(jnp.float32)).astype(
        jnp.bfloat16
    )
    send_x = jnp.dot(placed, flat_x, preferred_element_type=jnp.float32).astype(jnp.bfloat16)
    send_s = jnp.dot(placed, flat_scaled, preferred_element_type=jnp.float32).astype(jnp.bfloat16)
    send = jnp.concatenate([send_x, send_s], axis=1)
    got = lax.all_to_all(send, "expert", split_axis=0, concat_axis=0, tiled=True)
    rows = lax.all_gather(got, GROUP, axis=0, tiled=True)
    n_group = terms.shape[0] // count_tok
    pieces = terms.reshape(n_group, count_tok, 2 * model_width)
    pieces = lax.all_to_all(pieces, GROUP, split_axis=0, concat_axis=0, tiled=True)
    rows_x = rows[:, :model_width]
    rows_s = rows[:, model_width:]
    r_up, r_act, r_slope, r_hidden = forward_parts(rows_x, gate_cols, up_cols)
    r_gate, r_upg = grad_parts(rows_s, down_cols, r_up, r_act, r_slope)
    grad_gate = contract_rows(rows_x, r_gate).astype(jnp.bfloat16)[None]
    grad_up = contract_rows(rows_x, r_upg).astype(jnp.bfloat16)[None]
    grad_down_t = contract_rows(rows_s, r_hidden).astype(jnp.bfloat16)[None]
    pieces, grad_gate, grad_up, grad_down_t = lax.optimization_barrier(
        (pieces, grad_gate, grad_up, grad_down_t)
    )
    summed = jnp.sum(pieces.astype(jnp.float32), axis=0)
    expert_out = summed[:, :model_width].astype(jnp.bfloat16).astype(jnp.float32)
    mixed = (code_scale[:, 0:1] * expert_out + code_scale[:, 1:2] * expert_out).astype(
        jnp.bfloat16
    )
    input_grad = summed[:, model_width:].astype(jnp.bfloat16)
    return (mixed, input_grad, grad_gate, grad_up, grad_down_t)


def solution(mesh):
    rows = P(("dp", "expert", "tensor"), None)
    weights = P("expert", ("dp", "tensor"))
    grads = P("expert", None, ("dp", "tensor"))
    return jax.shard_map(
        shards,
        mesh=mesh,
        in_specs=(rows, rows, rows, rows, weights, weights, weights),
        out_specs=(rows, rows, grads, grads, grads),
        check_vma=False,
    )
```

```python
import jax
import jax.numpy as jnp
from jax import lax
from jax.sharding import PartitionSpec as P

GROUP = ("dp", "tensor")
PLANE = ("tensor", "dp")


def silu_parts(gate_pre):
    sigmoid_val = jax.nn.sigmoid(gate_pre)
    return (gate_pre * sigmoid_val, sigmoid_val * (1.0 + gate_pre * (1.0 - sigmoid_val)))


def contract_rows(left_side, right_side):
    return lax.dot_general(
        left_side, right_side, (((0,), (0,)), ((), ())), preferred_element_type=jnp.float32
    )


def contract_cols(left_side, right_side):
    return lax.dot_general(
        left_side, right_side, (((1,), (1,)), ((), ())), preferred_element_type=jnp.float32
    )


def forward_parts(rows_x, gate_cols, up_cols):
    gate_pre = jnp.dot(rows_x, gate_cols, preferred_element_type=jnp.float32)
    up_pre = jnp.dot(rows_x, up_cols, preferred_element_type=jnp.float32)
    activation, act_slope = silu_parts(gate_pre)
    hidden = (activation * up_pre).astype(jnp.bfloat16)
    return up_pre, activation, act_slope, hidden


def grad_parts(scaled, down_cols, up_pre, activation, act_slope):
    hidden_grad = jnp.dot(scaled, down_cols, preferred_element_type=jnp.float32)
    gate_grad = (hidden_grad * up_pre * act_slope).astype(jnp.bfloat16)
    up_grad = (hidden_grad * activation).astype(jnp.bfloat16)
    return gate_grad, up_grad


def shards(tokens, cotangent, routes, weight_codes, dense_gate, dense_up, dense_down_t):
    experts = lax.axis_size("expert")
    count_tok, model_width = tokens.shape
    hid = dense_gate.shape[1]
    capacity = 5 * count_tok // (2 * experts)
    slots_here = experts * capacity

    stacked = jnp.concatenate([dense_gate, dense_up, dense_down_t], axis=1)
    copies = jnp.broadcast_to(stacked[None], (experts,) + stacked.shape)
    full_cols = lax.all_to_all(copies, "expert", split_axis=0, concat_axis=0, tiled=True)
    full_cols = full_cols.reshape(-1, stacked.shape[1])
    gate_cols = full_cols[:, :hid]
    up_cols = full_cols[:, hid : 2 * hid]
    down_cols = full_cols[:, 2 * hid :]
    gate_up_cols = full_cols[:, : 2 * hid]

    code_scale = weight_codes.astype(jnp.float32) / 256.0
    pair_scale = code_scale[:, 0:1] + code_scale[:, 1:2]
    pair_scaled = (pair_scale * cotangent.astype(jnp.float32)).astype(jnp.bfloat16)
    home = jnp.concatenate([tokens, pair_scaled], axis=1)
    plane = lax.all_gather(home, PLANE, axis=0, tiled=True)
    plane_x = plane[:, :model_width]
    plane_s = plane[:, model_width:]

    up_pre, activation, act_slope, hidden = forward_parts(plane_x, gate_cols, up_cols)
    out_term = contract_cols(hidden, down_cols).astype(jnp.bfloat16)
    gate_grad, up_grad = grad_parts(plane_s, down_cols, up_pre, activation, act_slope)
    grad_term = contract_cols(jnp.concatenate([gate_grad, up_grad], axis=1), gate_up_cols)
    terms = jnp.concatenate([out_term, grad_term.astype(jnp.bfloat16)], axis=1)

    flat_route = routes.reshape(-1)
    flat_scale = weight_codes.reshape(-1).astype(jnp.float32) / 256.0
    onehot = (flat_route[:, None] == jnp.arange(experts, dtype=jnp.int32)[None, :]).astype(
        jnp.int32
    )
    earlier = jnp.cumsum(onehot, axis=0) - onehot
    slot_of = flat_route * capacity + jnp.sum(earlier * onehot, axis=1)
    placed = (slot_of[None, :] == jnp.arange(slots_here, dtype=jnp.int32)[:, None]).astype(
        jnp.bfloat16
    )
    flat_x = jnp.repeat(tokens, 2, axis=0)
    flat_scaled = (flat_scale[:, None] * jnp.repeat(cotangent, 2, axis=0).astype(jnp.float32)).astype(
        jnp.bfloat16
    )
    send_x = jnp.dot(placed, flat_x, preferred_element_type=jnp.float32).astype(jnp.bfloat16)
    send_s = jnp.dot(placed, flat_scaled, preferred_element_type=jnp.float32).astype(jnp.bfloat16)
    send = jnp.concatenate([send_x, send_s], axis=1)
    got = lax.all_to_all(send, "expert", split_axis=0, concat_axis=0, tiled=True)
    rows = lax.all_gather(got, GROUP, axis=0, tiled=True)
    n_group = terms.shape[0] // count_tok
    pieces = terms.reshape(n_group, count_tok, 2 * model_width)
    pieces = lax.all_to_all(pieces, PLANE, split_axis=0, concat_axis=0, tiled=True)
    rows_x = rows[:, :model_width]
    rows_s = rows[:, model_width:]
    r_up, r_act, r_slope, r_hidden = forward_parts(rows_x, gate_cols, up_cols)
    r_gate, r_upg = grad_parts(rows_s, down_cols, r_up, r_act, r_slope)
    grad_gate = contract_rows(rows_x, r_gate).astype(jnp.bfloat16)[None]
    grad_up = contract_rows(rows_x, r_upg).astype(jnp.bfloat16)[None]
    grad_down_t = contract_rows(rows_s, r_hidden).astype(jnp.bfloat16)[None]
    pieces, grad_gate, grad_up, grad_down_t = lax.optimization_barrier(
        (pieces, grad_gate, grad_up, grad_down_t)
    )
    summed = jnp.sum(pieces.astype(jnp.float32), axis=0)
    expert_out = summed[:, :model_width].astype(jnp.bfloat16).astype(jnp.float32)
    mixed = (code_scale[:, 0:1] * expert_out + code_scale[:, 1:2] * expert_out).astype(
        jnp.bfloat16
    )
    input_grad = summed[:, model_width:].astype(jnp.bfloat16)
    return (mixed, input_grad, grad_gate, grad_up, grad_down_t)


def solution(mesh):
    rows = P(("dp", "expert", "tensor"), None)
    weights = P("expert", ("dp", "tensor"))
    grads = P("expert", None, ("dp", "tensor"))
    return jax.shard_map(
        shards,
        mesh=mesh,
        in_specs=(rows, rows, rows, rows, weights, weights, weights),
        out_specs=(rows, rows, grads, grads, grads),
        check_vma=False,
    )
```

```python
import jax
import jax.numpy as jnp
from jax import lax
from jax.sharding import PartitionSpec as P

GROUP = ("dp", "tensor")


def silu_parts(gate_pre):
    sigmoid_val = jax.nn.sigmoid(gate_pre)
    return (gate_pre * sigmoid_val, sigmoid_val * (1.0 + gate_pre * (1.0 - sigmoid_val)))


def contract_rows(left_side, right_side):
    return lax.dot_general(
        left_side, right_side, (((0,), (0,)), ((), ())), preferred_element_type=jnp.float32
    )


def contract_cols(left_side, right_side):
    return lax.dot_general(
        left_side, right_side, (((1,), (1,)), ((), ())), preferred_element_type=jnp.float32
    )


def forward_parts(rows_x, gate_up_cols):
    both = jnp.dot(rows_x, gate_up_cols, preferred_element_type=jnp.float32)
    hid = gate_up_cols.shape[1] // 2
    gate_pre = both[:, :hid]
    up_pre = both[:, hid:]
    activation, act_slope = silu_parts(gate_pre)
    hidden = (activation * up_pre).astype(jnp.bfloat16)
    return up_pre, activation, act_slope, hidden


def grad_parts(scaled, down_cols, up_pre, activation, act_slope):
    hidden_grad = jnp.dot(scaled, down_cols, preferred_element_type=jnp.float32)
    gate_grad = (hidden_grad * up_pre * act_slope).astype(jnp.bfloat16)
    up_grad = (hidden_grad * activation).astype(jnp.bfloat16)
    return gate_grad, up_grad


def shards(tokens, cotangent, routes, weight_codes, dense_gate, dense_up, dense_down_t):
    experts = lax.axis_size("expert")
    count_tok, model_width = tokens.shape
    hid = dense_gate.shape[1]
    capacity = 5 * count_tok // (2 * experts)
    slots_here = experts * capacity

    stacked = jnp.concatenate([dense_gate, dense_up, dense_down_t], axis=1)
    copies = jnp.broadcast_to(stacked[None], (experts,) + stacked.shape)
    full_cols = lax.all_to_all(copies, "expert", split_axis=0, concat_axis=0, tiled=True)
    full_cols = full_cols.reshape(-1, stacked.shape[1])
    gate_cols = full_cols[:, :hid]
    up_cols = full_cols[:, hid : 2 * hid]
    down_cols = full_cols[:, 2 * hid :]
    gate_up_cols = full_cols[:, : 2 * hid]

    code_scale = weight_codes.astype(jnp.float32) / 256.0
    pair_scale = code_scale[:, 0:1] + code_scale[:, 1:2]
    pair_scaled = (pair_scale * cotangent.astype(jnp.float32)).astype(jnp.bfloat16)
    home = jnp.concatenate([tokens, pair_scaled], axis=1)
    plane = lax.all_gather(home, GROUP, axis=0, tiled=True)
    plane_x = plane[:, :model_width]
    plane_s = plane[:, model_width:]

    up_pre, activation, act_slope, hidden = forward_parts(plane_x, gate_up_cols)
    out_term = contract_cols(hidden, down_cols).astype(jnp.bfloat16)
    gate_grad, up_grad = grad_parts(plane_s, down_cols, up_pre, activation, act_slope)
    grad_term = contract_cols(jnp.concatenate([gate_grad, up_grad], axis=1), gate_up_cols)
    terms = jnp.concatenate([out_term, grad_term.astype(jnp.bfloat16)], axis=1)

    flat_route = routes.reshape(-1)
    flat_scale = weight_codes.reshape(-1).astype(jnp.float32) / 256.0
    onehot = (flat_route[:, None] == jnp.arange(experts, dtype=jnp.int32)[None, :]).astype(
        jnp.int32
    )
    earlier = jnp.cumsum(onehot, axis=0) - onehot
    slot_of = flat_route * capacity + jnp.sum(earlier * onehot, axis=1)
    placed = (slot_of[None, :] == jnp.arange(slots_here, dtype=jnp.int32)[:, None]).astype(
        jnp.bfloat16
    )
    flat_x = jnp.repeat(tokens, 2, axis=0)
    flat_scaled = (flat_scale[:, None] * jnp.repeat(cotangent, 2, axis=0).astype(jnp.float32)).astype(
        jnp.bfloat16
    )
    send_x = jnp.dot(placed, flat_x, preferred_element_type=jnp.float32).astype(jnp.bfloat16)
    send_s = jnp.dot(placed, flat_scaled, preferred_element_type=jnp.float32).astype(jnp.bfloat16)
    send = jnp.concatenate([send_x, send_s], axis=1)
    got = lax.all_to_all(send, "expert", split_axis=0, concat_axis=0, tiled=True)
    rows = lax.all_gather(got, GROUP, axis=0, tiled=True)
    n_group = terms.shape[0] // count_tok
    pieces = terms.reshape(n_group, count_tok, 2 * model_width)
    pieces = lax.all_to_all(pieces, GROUP, split_axis=0, concat_axis=0, tiled=True)
    rows_x = rows[:, :model_width]
    rows_s = rows[:, model_width:]
    r_up, r_act, r_slope, r_hidden = forward_parts(rows_x, gate_up_cols)
    r_gate, r_upg = grad_parts(rows_s, down_cols, r_up, r_act, r_slope)
    grad_gate = contract_rows(rows_x, r_gate).astype(jnp.bfloat16)[None]
    grad_up = contract_rows(rows_x, r_upg).astype(jnp.bfloat16)[None]
    grad_down_t = contract_rows(rows_s, r_hidden).astype(jnp.bfloat16)[None]
    pieces, grad_gate, grad_up, grad_down_t = lax.optimization_barrier(
        (pieces, grad_gate, grad_up, grad_down_t)
    )
    summed = jnp.sum(pieces.astype(jnp.float32), axis=0)
    expert_out = summed[:, :model_width].astype(jnp.bfloat16).astype(jnp.float32)
    mixed = (code_scale[:, 0:1] * expert_out + code_scale[:, 1:2] * expert_out).astype(
        jnp.bfloat16
    )
    input_grad = summed[:, model_width:].astype(jnp.bfloat16)
    return (mixed, input_grad, grad_gate, grad_up, grad_down_t)


def solution(mesh):
    rows = P(("dp", "expert", "tensor"), None)
    weights = P("expert", ("dp", "tensor"))
    grads = P("expert", None, ("dp", "tensor"))
    return jax.shard_map(
        shards,
        mesh=mesh,
        in_specs=(rows, rows, rows, rows, weights, weights, weights),
        out_specs=(rows, rows, grads, grads, grads),
        check_vma=False,
    )
```

```python
import jax
import jax.numpy as jnp
from jax import lax
from jax.sharding import PartitionSpec as P

GROUP = ("dp", "tensor")


def silu_parts(gate_pre):
    sigmoid_val = jax.nn.sigmoid(gate_pre)
    return (gate_pre * sigmoid_val, sigmoid_val * (1.0 + gate_pre * (1.0 - sigmoid_val)))


def contract_rows(left_side, right_side):
    return lax.dot_general(
        left_side, right_side, (((0,), (0,)), ((), ())), preferred_element_type=jnp.float32
    )


def contract_cols(left_side, right_side):
    return lax.dot_general(
        left_side, right_side, (((1,), (1,)), ((), ())), preferred_element_type=jnp.float32
    )


def forward_parts(rows_x, gate_cols, up_cols):
    gate_pre = jnp.dot(rows_x, gate_cols, preferred_element_type=jnp.float32)
    up_pre = jnp.dot(rows_x, up_cols, preferred_element_type=jnp.float32)
    activation, act_slope = silu_parts(gate_pre)
    hidden = (activation * up_pre).astype(jnp.bfloat16)
    return up_pre, activation, act_slope, hidden


def grad_parts(scaled, down_cols, up_pre, activation, act_slope):
    hidden_grad = jnp.dot(scaled, down_cols, preferred_element_type=jnp.float32)
    gate_grad = (hidden_grad * up_pre * act_slope).astype(jnp.bfloat16)
    up_grad = (hidden_grad * activation).astype(jnp.bfloat16)
    return gate_grad, up_grad


def shards(tokens, cotangent, routes, weight_codes, dense_gate, dense_up, dense_down_t):
    experts = lax.axis_size("expert")
    count_tok, model_width = tokens.shape
    hid = dense_gate.shape[1]
    capacity = 5 * count_tok // (2 * experts)
    slots_here = experts * capacity

    stacked = jnp.concatenate([dense_gate, dense_up, dense_down_t], axis=1)
    copies = jnp.broadcast_to(stacked[None], (experts,) + stacked.shape)
    full_cols = lax.all_to_all(copies, "expert", split_axis=0, concat_axis=0, tiled=True)
    full_cols = full_cols.reshape(-1, stacked.shape[1])
    gate_cols = full_cols[:, :hid]
    up_cols = full_cols[:, hid : 2 * hid]
    down_cols = full_cols[:, 2 * hid :]
    gate_up_cols = full_cols[:, : 2 * hid]

    code_scale = weight_codes.astype(jnp.float32) / 256.0
    pair_scale = code_scale[:, 0:1] + code_scale[:, 1:2]
    pair_scaled = (pair_scale * cotangent.astype(jnp.float32)).astype(jnp.bfloat16)
    home = jnp.concatenate([tokens, pair_scaled], axis=1)
    plane = lax.all_gather(home, GROUP, axis=0, tiled=True)
    plane_x = plane[:, :model_width]
    plane_s = plane[:, model_width:]

    up_pre, activation, act_slope, hidden = forward_parts(plane_x, gate_cols, up_cols)
    out_term = contract_cols(hidden, down_cols).astype(jnp.bfloat16)
    gate_grad, up_grad = grad_parts(plane_s, down_cols, up_pre, activation, act_slope)
    grad_term = contract_cols(jnp.concatenate([gate_grad, up_grad], axis=1), gate_up_cols)
    terms = jnp.concatenate([out_term, grad_term.astype(jnp.bfloat16)], axis=1)

    flat_route = routes.reshape(-1)
    flat_scale = weight_codes.reshape(-1).astype(jnp.float32) / 256.0
    onehot = (flat_route[:, None] == jnp.arange(experts, dtype=jnp.int32)[None, :]).astype(
        jnp.int32
    )
    earlier = jnp.cumsum(onehot, axis=0) - onehot
    slot_of = flat_route * capacity + jnp.sum(earlier * onehot, axis=1)
    placed = (slot_of[None, :] == jnp.arange(slots_here, dtype=jnp.int32)[:, None]).astype(
        jnp.bfloat16
    )
    flat_x = jnp.repeat(tokens, 2, axis=0)
    flat_scaled = (flat_scale[:, None] * jnp.repeat(cotangent, 2, axis=0).astype(jnp.float32)).astype(
        jnp.bfloat16
    )
    send_x = jnp.dot(placed, flat_x, preferred_element_type=jnp.float32).astype(jnp.bfloat16)
    send_s = jnp.dot(placed, flat_scaled, preferred_element_type=jnp.float32).astype(jnp.bfloat16)
    send = jnp.concatenate([send_x, send_s], axis=1)
    got = lax.all_to_all(send, "expert", split_axis=0, concat_axis=0, tiled=True)
    rows = lax.all_gather(got, GROUP, axis=0, tiled=True)
    n_group = terms.shape[0] // count_tok
    pieces = terms.reshape(n_group, count_tok, 2 * model_width)
    pieces = lax.all_to_all(pieces, GROUP, split_axis=0, concat_axis=0, tiled=True)
    rows_x = rows[:, :model_width]
    rows_s = rows[:, model_width:]
    r_up, r_act, r_slope, r_hidden = forward_parts(rows_x, gate_cols, up_cols)
    r_gate, r_upg = grad_parts(rows_s, down_cols, r_up, r_act, r_slope)
    grad_gate = contract_rows(rows_x, r_gate).astype(jnp.bfloat16)[None]
    grad_up = contract_rows(rows_x, r_upg).astype(jnp.bfloat16)[None]
    grad_down_t = contract_rows(rows_s, r_hidden).astype(jnp.bfloat16)[None]
    pieces, grad_gate, grad_up, grad_down_t = lax.optimization_barrier(
        (pieces, grad_gate, grad_up, grad_down_t)
    )
    expert_out = jnp.sum(pieces[:, :, :model_width].astype(jnp.float32), axis=0)
    expert_out = expert_out.astype(jnp.bfloat16).astype(jnp.float32)
    mixed = (code_scale[:, 0:1] * expert_out + code_scale[:, 1:2] * expert_out).astype(
        jnp.bfloat16
    )
    input_grad = jnp.sum(pieces[:, :, model_width:].astype(jnp.float32), axis=0).astype(
        jnp.bfloat16
    )
    return (mixed, input_grad, grad_gate, grad_up, grad_down_t)


def solution(mesh):
    rows = P(("dp", "expert", "tensor"), None)
    weights = P("expert", ("dp", "tensor"))
    grads = P("expert", None, ("dp", "tensor"))
    return jax.shard_map(
        shards,
        mesh=mesh,
        in_specs=(rows, rows, rows, rows, weights, weights, weights),
        out_specs=(rows, rows, grads, grads, grads),
        check_vma=False,
    )
```
